128 devices in a mesh: node: 4 (over y), freq: 32 (over z, x, core).
Axes of the slice: x: 4, y: 4, z: 4, core: 2. Of those that a mesh axis runs over, the one named last changes fastest.
Arguments:
- first_vector: float32 [2, 256, 512, 256], P(None, 'freq', 'node'), may hold values from -6 to 6
- second_vector: float32 [2, 256, 512, 256], P(None, 'freq', 'node'), may hold values from -6 to 6
- conductance: float32 [2, 256, 512, 256], P(None, 'freq', 'node'), may hold values from 0.1 to 2
- terminals: int32 [512, 3], replicated, may hold values from 0 to 127
- pattern: int32 [16, 3], P('node'), may hold values from 0 to 3, all different within a row
- conduct_blocks: float32 [16, 3, 32, 32], P('node'), may hold values from -0.625 to 0.625
- capacit_blocks: float32 [16, 3, 32, 32], P('node'), may hold values from -0.625 to 0.625
Outputs:
- first_product: float32 [2, 256, 512, 256], P(None, 'freq', 'node')
- second_product: float32 [2, 256, 512, 256], P(None, 'freq', 'node')
The draws below stay inside these ranges and needn't reach their ends.
Inputs may be any that keep to these rules, and one draw needn't show every extreme that they name: `terminals`: drain and source indices count within the transistor's own node block; transistor j of a node block (j counted within the block) takes its gate from node block j // 32, so every node block draws exactly 32 gates from every node block. `pattern`: each row names 3 different column blocks, counted within the row's own node block.
All inputs are finite; a program needn't handle non-finite values.
Results may differ from the reference program's by a relative error of at most 0.000058.
Values sent between devices are 32-bit elements; how exact they have to be, the bound alone decides.
No kernel may reach another device: no remote copies, remote signals or barrier semaphores. Data moves between devices by JAX's collectives and lax.ppermute only.
A program may use at most 128 MiB of HBM per device.

```python
import math
import jax
import jax.numpy as jnp
from jax import lax

NODE_DEV = 128
OUTER = 256
INNER = 256
BS = 32
NNZ = 3
NODES = 512
BLOCKS = 16
N_NODE = 4


def plant(values, stream_key, least, largest):
    longest = values.shape.index(max(values.shape))
    spots = []
    for shift in (0, 1):
        where = [jax.random.randint(jax.random.fold_in(stream_key, axis), (), 0, length) for axis, length in enumerate(values.shape)]
        where[longest] = (where[longest] + shift) % values.shape[longest]
        spots.append(tuple(where))
    return values.at[spots[0]].set(least).at[spots[1]].set(largest)


def steps_of(own_key, shape, pieces, smallest, largest):
    loudness, own = 1.0, jax.random.fold_in(own_key, 6)
    for axis_at, shards_of in pieces:
        draws = jnp.exp(jax.random.uniform(jax.random.fold_in(own, axis_at), (shards_of,), jnp.float32, smallest / len(pieces), largest / len(pieces)))
        loudness = loudness * jnp.repeat(draws, shape[axis_at] // shards_of).reshape([-1 if axis == axis_at else 1 for axis in range(len(shape))])
    return loudness


def choose_distinct(key, rows, amount, top, lift):
    order = jax.random.permutation(jax.random.fold_in(key, 1), amount)
    favour = order
    for power in range(3):
        favour = favour * favour // amount
    favour = favour * lift // amount
    chance = jax.random.randint(jax.random.fold_in(key, 2), (rows, amount), 0, 4096) + favour
    sure = jax.random.permutation(jax.random.fold_in(key, 3), rows)[jnp.arange(amount) % rows]
    chance = jnp.where(jnp.arange(rows)[:, None] == sure[None, :], 1 << 14, chance)
    priority = chance * amount + jnp.arange(amount)
    return lax.top_k(priority.astype(jnp.int32), top)[1].astype(jnp.int32)


def centred(rng, shape, width, bound, cuts=(), held_as=jnp.bfloat16):
    level = steps_of(rng, shape, cuts, -0.22, 0.18) if cuts else 1.0
    values = jax.random.normal(rng, shape, jnp.float32) * width * level
    return jnp.minimum(jnp.maximum(values, -bound), bound).astype(held_as)


def setup_inputs(seed: int = 0) -> dict:
    arg_keys = jax.random.split(jax.random.key(seed), 8)
    first_vector = centred(arg_keys[0], (2, OUTER, NODES, INNER), 1.0, 6.0, ((1, 32), (2, 4)), jnp.float32)
    second_vector = centred(arg_keys[1], (2, OUTER, NODES, INNER), 1.0, 6.0, ((1, 32), (2, 4)), jnp.float32)
    conductance = jnp.clip(jnp.exp(math.log(2.0) - 2.9957323 * jax.random.uniform(arg_keys[2], (2, INNER, NODES, OUTER), jnp.float32) ** steps_of(arg_keys[2], (2, INNER, NODES, OUTER), ((1, 32), (2, 4)), -0.2, 0.2)), 0.1, 2.0)
    terminals = plant(jax.random.randint(arg_keys[3], (NODES, 3), 0, NODE_DEV), jax.random.fold_in(arg_keys[3], 1), 0, NODE_DEV - 1).astype(jnp.int32)
    pattern = choose_distinct(arg_keys[4], BLOCKS, NODE_DEV // BS, NNZ, 0)
    conduct_blocks = centred(arg_keys[5], (BLOCKS, NNZ, BS, BS), (NNZ * BS) ** -0.5, 0.625, ((0, 4),), jnp.float32)
    capacit_blocks = centred(arg_keys[6], (BLOCKS, NNZ, BS, BS), (NNZ * BS) ** -0.5, 0.625, ((0, 4),), jnp.float32)
    return dict(first_vector=first_vector, second_vector=second_vector, conductance=conductance, terminals=terminals, pattern=pattern, conduct_blocks=conduct_blocks, capacit_blocks=capacit_blocks)


def reference(first_vector, second_vector, conductance, terminals, pattern, conduct_blocks, capacit_blocks):
    node_dev = NODE_DEV
    nodes = NODES
    samples = OUTER * INNER
    capacity = node_dev // N_NODE
    block_count = node_dev // BS
    device = jnp.arange(nodes, dtype=jnp.int32)
    group = device // node_dev
    slot = device % node_dev
    drain = group * node_dev + terminals[:, 0]
    source = group * node_dev + terminals[:, 1]
    gate = (slot // capacity) * node_dev + terminals[:, 2]
    trans_g = conductance[0].transpose(1, 2, 0).reshape(nodes, samples)
    output_g = conductance[1].transpose(1, 2, 0).reshape(nodes, samples)
    pattern_hot = (pattern[:, :, None] == jnp.arange(block_count, dtype=jnp.int32)[None, None, :]).astype(jnp.float32)
    conduct_dense = jnp.einsum("bjc,bjrs->brcs", pattern_hot, conduct_blocks, precision=lax.Precision.HIGHEST)
    conduct_dense = conduct_dense.reshape(N_NODE, node_dev, node_dev)
    capacit_dense = jnp.einsum("bjc,bjrs->brcs", pattern_hot, capacit_blocks, precision=lax.Precision.HIGHEST)
    capacit_dense = capacit_dense.reshape(N_NODE, node_dev, node_dev)
    bins = jnp.arange(samples, dtype=jnp.int32)
    signed = jnp.where(bins < samples // 2, bins, bins - samples)
    angular = (signed.astype(jnp.float32) * (2.0 * math.pi / samples)).reshape(INNER, OUTER).T[:, None, :]

    def apply_mna(dense, part):
        grouped = part.reshape(OUTER, N_NODE, node_dev, INNER)
        result = jnp.einsum("grs,agsb->agrb", dense, grouped, precision=lax.Precision.HIGHEST)
        return result.reshape(OUTER, nodes, INNER)

    def product(vector):
        spectrum = lax.complex(vector[0], vector[1]).transpose(1, 2, 0).reshape(nodes, samples)
        signal = jnp.fft.ifft(spectrum, axis=1)
        current = trans_g * (signal[gate] - signal[source]) + output_g * (signal[drain] - signal[source])
        injected = jnp.zeros_like(signal).at[drain].add(current).at[source].add(-current)
        response = jnp.fft.fft(injected, axis=1).reshape(nodes, INNER, OUTER).transpose(2, 0, 1)
        real_out = apply_mna(conduct_dense, vector[0]) - angular * apply_mna(capacit_dense, vector[1]) + jnp.real(response)
        imag_out = apply_mna(conduct_dense, vector[1]) + angular * apply_mna(capacit_dense, vector[0]) + jnp.imag(response)
        return jnp.stack([real_out, imag_out])

    return (product(first_vector), product(second_vector))
```

```python
import math

import jax
import jax.numpy as jnp
from jax import lax
from jax.sharding import PartitionSpec as P

dft_precision = lax.Precision.HIGH
pick_precision = lax.Precision.HIGH
mna_precision = lax.Precision.HIGH


def contract(form, left, right, precision):
    return jnp.einsum(form, left, right, precision=precision)


def cos_sin(first, second, length):
    angle = (first[:, None] * second[None, :] % length).astype(jnp.float32) * (
        2.0 * math.pi / length
    )
    return (jnp.cos(angle), jnp.sin(angle))


def body(
    first_vector, second_vector, conductance, terminals, pattern, conduct_blocks, capacit_blocks
):
    freq_count = lax.axis_size("freq")
    groups = lax.axis_size("node")
    local_bins = first_vector.shape[1]
    node_dev = first_vector.shape[2]
    inner_size = first_vector.shape[3]
    outer_size = local_bins * freq_count
    samples = outer_size * inner_size
    local_steps = inner_size // freq_count
    capacity = node_dev // groups
    freq_index = lax.axis_index("freq")
    node_index = lax.axis_index("node")
    bin_first = freq_index * local_bins + jnp.arange(local_bins, dtype=jnp.int32)
    step_first = freq_index * local_steps + jnp.arange(local_steps, dtype=jnp.int32)
    inner_range = jnp.arange(inner_size, dtype=jnp.int32)
    outer_range = jnp.arange(outer_size, dtype=jnp.int32)
    inner_cos, inner_sin = cos_sin(inner_range, inner_range, inner_size)
    outer_cos, outer_sin = cos_sin(outer_range, outer_range, outer_size)
    back_cos, back_sin = cos_sin(inner_range, bin_first, samples)
    fore_cos, fore_sin = cos_sin(step_first, outer_range, samples)
    scale = 1.0 / samples

    node_ids = jnp.arange(node_dev, dtype=jnp.int32)
    own_rows = lax.dynamic_slice_in_dim(terminals, node_index * node_dev, node_dev, 0)
    drain_hot = (own_rows[:, 0, None] == node_ids[None, :]).astype(jnp.float32)
    source_hot = (own_rows[:, 1, None] == node_ids[None, :]).astype(jnp.float32)
    incidence = (drain_hot - source_hot).T
    arranged = terminals.reshape(groups, groups, capacity, 3)
    wanted = lax.dynamic_index_in_dim(arranged, node_index, axis=1, keepdims=False)
    gate_hot = (wanted[:, :, 2, None] == node_ids[None, None, :]).astype(jnp.float32)
    gate_hot = gate_hot.reshape(groups * capacity, node_dev)

    trans_g = conductance[0]
    output_g = conductance[1]

    block_size = conduct_blocks.shape[2]
    block_count = node_dev // block_size
    pattern_hot = (
        pattern[:, :, None] == jnp.arange(block_count, dtype=jnp.int32)[None, None, :]
    ).astype(jnp.float32)
    conduct_dense = contract(
        "bjc,bjrs->brcs", pattern_hot, conduct_blocks, lax.Precision.HIGHEST
    ).reshape(node_dev, node_dev)
    capacit_dense = contract(
        "bjc,bjrs->brcs", pattern_hot, capacit_blocks, lax.Precision.HIGHEST
    ).reshape(node_dev, node_dev)
    bin_index = bin_first[:, None] + outer_size * inner_range[None, :]
    signed = jnp.where(bin_index < samples // 2, bin_index, bin_index - samples)
    angular = (signed.astype(jnp.float32) * (2.0 * math.pi / samples))[:, None, :]

    def product(vector):
        v_real, v_imag = vector[0], vector[1]
        mix_real = contract("anb,bm->man", v_real, inner_cos, dft_precision) - contract(
            "anb,bm->man", v_imag, inner_sin, dft_precision
        )
        mix_imag = contract("anb,bm->man", v_real, inner_sin, dft_precision) + contract(
            "anb,bm->man", v_imag, inner_cos, dft_precision
        )
        tc = back_cos[:, :, None]
        ts = back_sin[:, :, None]
        spread = lax.all_to_all(
            jnp.stack([mix_real * tc - mix_imag * ts, mix_real * ts + mix_imag * tc]),
            "freq",
            split_axis=1,
            concat_axis=2,
            tiled=True,
        )
        s_real, s_imag = spread[0], spread[1]
        sig_real = (
            contract("man,al->mnl", s_real, outer_cos, dft_precision)
            - contract("man,al->mnl", s_imag, outer_sin, dft_precision)
        ) * scale
        sig_imag = (
            contract("man,al->mnl", s_real, outer_sin, dft_precision)
            + contract("man,al->mnl", s_imag, outer_cos, dft_precision)
        ) * scale
        signal = jnp.stack([sig_real, sig_imag])
        outgoing = contract("pn,cmnl->cmpl", gate_hot, signal, pick_precision)
        at_gate = lax.all_to_all(
            outgoing, "node", split_axis=2, concat_axis=2, tiled=True
        )
        at_drain = contract("dn,cmnl->cmdl", drain_hot, signal, pick_precision)
        at_source = contract("dn,cmnl->cmdl", source_hot, signal, pick_precision)
        current = trans_g * (at_gate - at_source) + output_g * (at_drain - at_source)
        injected = contract("nd,cmdl->cmnl", incidence, current, pick_precision)
        i_real, i_imag = injected[0], injected[1]
        turn_real = contract("mnl,la->mna", i_real, outer_cos, dft_precision) + contract(
            "mnl,la->mna", i_imag, outer_sin, dft_precision
        )
        turn_imag = contract("mnl,la->mna", i_imag, outer_cos, dft_precision) - contract(
            "mnl,la->mna", i_real, outer_sin, dft_precision
        )
        fc = fore_cos[:, None, :]
        fs = fore_sin[:, None, :]
        collected = lax.all_to_all(
            jnp.stack([turn_real * fc + turn_imag * fs, turn_imag * fc - turn_real * fs]),
            "freq",
            split_axis=3,
            concat_axis=1,
            tiled=True,
        )
        c_real, c_imag = collected[0], collected[1]
        out_real = contract("mna,mb->anb", c_real, inner_cos, dft_precision) + contract(
            "mna,mb->anb", c_imag, inner_sin, dft_precision
        )
        out_imag = contract("mna,mb->anb", c_imag, inner_cos, dft_precision) - contract(
            "mna,mb->anb", c_real, inner_sin, dft_precision
        )
        real_out = contract("rs,asb->arb", conduct_dense, v_real, mna_precision) - angular * contract(
            "rs,asb->arb", capacit_dense, v_imag, mna_precision
        )
        imag_out = contract("rs,asb->arb", conduct_dense, v_imag, mna_precision) + angular * contract(
            "rs,asb->arb", capacit_dense, v_real, mna_precision
        )
        return jnp.stack([real_out + out_real, imag_out + out_imag])

    return (product(first_vector), product(second_vector))


def solution(mesh):
    return jax.shard_map(
        body,
        mesh=mesh,
        in_specs=(
            P(None, "freq", "node", None),
            P(None, "freq", "node", None),
            P(None, "freq", "node", None),
            P(),
            P("node", None),
            P("node", None, None, None),
            P("node", None, None, None),
        ),
        out_specs=(P(None, "freq", "node", None), P(None, "freq", "node", None)),
        check_vma=False,
    )
```

```python
import math

import jax
import jax.numpy as jnp
from jax import lax
from jax.sharding import PartitionSpec as P

dft_precision = lax.Precision.HIGH
pick_precision = lax.Precision.HIGH
mna_precision = lax.Precision.HIGH


def contract(form, left, right, precision):
    return jnp.einsum(form, left, right, precision=precision)


def cos_sin(first, second, length):
    angle = (first[:, None] * second[None, :] % length).astype(jnp.float32) * (
        2.0 * math.pi / length
    )
    return (jnp.cos(angle), jnp.sin(angle))


def body(
    first_vector, second_vector, conductance, terminals, pattern, conduct_blocks, capacit_blocks
):
    freq_count = lax.axis_size("freq")
    groups = lax.axis_size("node")
    local_bins = first_vector.shape[1]
    node_dev = first_vector.shape[2]
    inner_size = first_vector.shape[3]
    outer_size = local_bins * freq_count
    samples = outer_size * inner_size
    local_steps = inner_size // freq_count
    capacity = node_dev // groups
    freq_index = lax.axis_index("freq")
    node_index = lax.axis_index("node")
    bin_first = freq_index * local_bins + jnp.arange(local_bins, dtype=jnp.int32)
    step_first = freq_index * local_steps + jnp.arange(local_steps, dtype=jnp.int32)
    inner_range = jnp.arange(inner_size, dtype=jnp.int32)
    outer_range = jnp.arange(outer_size, dtype=jnp.int32)
    inner_cos, inner_sin = cos_sin(inner_range, inner_range, inner_size)
    outer_cos, outer_sin = cos_sin(outer_range, outer_range, outer_size)
    back_cos, back_sin = cos_sin(inner_range, bin_first, samples)
    fore_cos, fore_sin = cos_sin(step_first, outer_range, samples)
    scale = 1.0 / samples
    inv_inner = (
        jnp.stack([inner_cos, inner_sin], axis=1),
        jnp.stack([-inner_sin, inner_cos], axis=1),
    )
    inv_outer = (
        jnp.stack([outer_cos, outer_sin], axis=1) * scale,
        jnp.stack([-outer_sin, outer_cos], axis=1) * scale,
    )
    fwd_outer = (
        jnp.stack([outer_cos, -outer_sin], axis=1),
        jnp.stack([outer_sin, outer_cos], axis=1),
    )
    fwd_inner = (
        jnp.stack([inner_cos, -inner_sin], axis=1),
        jnp.stack([inner_sin, inner_cos], axis=1),
    )
    back_sign = jnp.array([-1.0, 1.0], jnp.float32)[:, None, None, None]
    fore_sign = jnp.array([1.0, -1.0], jnp.float32)[:, None, None, None]
    back_c = back_cos[None, :, :, None]
    back_s = back_sin[None, :, :, None] * back_sign
    fore_c = fore_cos[None, :, None, :]
    fore_s = fore_sin[None, :, None, :] * fore_sign

    node_ids = jnp.arange(node_dev, dtype=jnp.int32)
    turns = jnp.arange(groups, dtype=jnp.int32)
    recv_blocks = (node_index + turns) % groups
    send_blocks = (node_index - turns) % groups
    own_rows = lax.dynamic_slice_in_dim(terminals, node_index * node_dev, node_dev, 0)
    own_rot = own_rows.reshape(groups, capacity, 3)[recv_blocks].reshape(node_dev, 3)
    drain_hot = (own_rot[:, 0, None] == node_ids[None, :]).astype(jnp.float32)
    source_hot = (own_rot[:, 1, None] == node_ids[None, :]).astype(jnp.float32)
    incidence = drain_hot - source_hot
    arranged = terminals.reshape(groups, groups, capacity, 3)
    wanted = lax.dynamic_index_in_dim(arranged, node_index, axis=1, keepdims=False)
    wanted = wanted[send_blocks].reshape(node_dev, 3)
    gate_hot = (wanted[:, 2, None] == node_ids[None, :]).astype(jnp.float32)
    picks = jnp.concatenate([gate_hot, incidence, source_hot], axis=0)

    cond_blocks = conductance.reshape(
        conductance.shape[0], conductance.shape[1], groups, capacity, conductance.shape[3]
    )
    cond_rot = jnp.concatenate(
        [
            lax.dynamic_slice_in_dim(cond_blocks, recv_blocks[s], 1, axis=2)
            for s in range(groups)
        ],
        axis=2,
    ).reshape(conductance.shape)
    trans_g = cond_rot[0]
    output_g = cond_rot[1]

    block_size = conduct_blocks.shape[2]
    block_count = node_dev // block_size
    pattern_hot = (
        pattern[:, :, None] == jnp.arange(block_count, dtype=jnp.int32)[None, None, :]
    ).astype(jnp.float32)
    conduct_dense = contract(
        "bjc,bjrs->brcs", pattern_hot, conduct_blocks, lax.Precision.HIGHEST
    ).reshape(node_dev, node_dev)
    capacit_dense = contract(
        "bjc,bjrs->brcs", pattern_hot, capacit_blocks, lax.Precision.HIGHEST
    ).reshape(node_dev, node_dev)
    mna = jnp.stack([conduct_dense, capacit_dense])
    bin_index = bin_first[:, None] + outer_size * inner_range[None, :]
    signed = jnp.where(bin_index < samples // 2, bin_index, bin_index - samples)
    angular = (signed.astype(jnp.float32) * (2.0 * math.pi / samples))[:, None, :]

    def complex_dft(form, parts, mats):
        return contract(form, parts[0], mats[0], dft_precision) + contract(
            form, parts[1], mats[1], dft_precision
        )

    def product(vector):
        mixed = complex_dft("anb,bkm->kman", (vector[0], vector[1]), inv_inner)
        spread = lax.all_to_all(
            mixed * back_c + mixed[::-1] * back_s,
            "freq",
            split_axis=1,
            concat_axis=2,
            tiled=True,
        )
        signal = complex_dft("man,akl->kmnl", (spread[0], spread[1]), inv_outer)
        picked = contract("dn,kmnl->kmdl", picks, signal, pick_precision)
        outgoing = picked[:, :, :node_dev]
        pieces = [outgoing[:, :, :capacity]]
        for s in range(1, groups):
            pieces.append(
                lax.ppermute(
                    outgoing[:, :, s * capacity : (s + 1) * capacity],
                    "node",
                    [(i, (i - s) % groups) for i in range(groups)],
                )
            )
        at_gate = jnp.concatenate(pieces, axis=2)
        drain_less_source = picked[:, :, node_dev : 2 * node_dev]
        at_source = picked[:, :, 2 * node_dev :]
        current = trans_g * (at_gate - at_source) + output_g * drain_less_source
        injected = contract("dn,kmdl->kmnl", incidence, current, pick_precision)
        turned = complex_dft("mnl,lka->kmna", (injected[0], injected[1]), fwd_outer)
        collected = lax.all_to_all(
            turned * fore_c + turned[::-1] * fore_s,
            "freq",
            split_axis=3,
            concat_axis=1,
            tiled=True,
        )
        response = complex_dft("mna,mkb->kanb", (collected[0], collected[1]), fwd_inner)
        from_real = contract("jrs,asb->jarb", mna, vector[0], mna_precision)
        from_imag = contract("jrs,asb->jarb", mna, vector[1], mna_precision)
        return jnp.stack(
            [
                response[0] + from_real[0] - angular * from_imag[1],
                response[1] + from_imag[0] + angular * from_real[1],
            ]
        )

    return (product(first_vector), product(second_vector))


def solution(mesh):
    return jax.shard_map(
        body,
        mesh=mesh,
        in_specs=(
            P(None, "freq", "node", None),
            P(None, "freq", "node", None),
            P(None, "freq", "node", None),
            P(),
            P("node", None),
            P("node", None, None, None),
            P("node", None, None, None),
        ),
        out_specs=(P(None, "freq", "node", None), P(None, "freq", "node", None)),
        check_vma=False,
    )
```

```python
import math

import jax
import jax.numpy as jnp
from jax import lax
from jax.sharding import PartitionSpec as P

dft_precision = lax.Precision.HIGH
pick_precision = lax.Precision.HIGH
mna_precision = lax.Precision.HIGH


def contract(form, left, right, precision):
    return jnp.einsum(form, left, right, precision=precision)


def cos_sin(first, second, length):
    angle = (first[:, None] * second[None, :] % length).astype(jnp.float32) * (
        2.0 * math.pi / length
    )
    return (jnp.cos(angle), jnp.sin(angle))


def body(
    first_vector, second_vector, conductance, terminals, pattern, conduct_blocks, capacit_blocks
):
    freq_count = lax.axis_size("freq")
    groups = lax.axis_size("node")
    local_bins = first_vector.shape[1]
    node_dev = first_vector.shape[2]
    inner_size = first_vector.shape[3]
    outer_size = local_bins * freq_count
    samples = outer_size * inner_size
    local_steps = inner_size // freq_count
    capacity = node_dev // groups
    freq_index = lax.axis_index("freq")
    node_index = lax.axis_index("node")
    bin_first = freq_index * local_bins + jnp.arange(local_bins, dtype=jnp.int32)
    step_first = freq_index * local_steps + jnp.arange(local_steps, dtype=jnp.int32)
    inner_range = jnp.arange(inner_size, dtype=jnp.int32)
    outer_range = jnp.arange(outer_size, dtype=jnp.int32)
    inner_cos, inner_sin = cos_sin(inner_range, inner_range, inner_size)
    outer_cos, outer_sin = cos_sin(outer_range, outer_range, outer_size)
    back_cos, back_sin = cos_sin(inner_range, bin_first, samples)
    fore_cos, fore_sin = cos_sin(step_first, outer_range, samples)
    scale = 1.0 / samples
    inv_inner = (
        jnp.stack([inner_cos, inner_sin], axis=1),
        jnp.stack([-inner_sin, inner_cos], axis=1),
    )
    inv_outer = (
        jnp.stack([outer_cos, outer_sin], axis=1) * scale,
        jnp.stack([-outer_sin, outer_cos], axis=1) * scale,
    )
    fwd_outer = (
        jnp.stack([outer_cos, -outer_sin], axis=1),
        jnp.stack([outer_sin, outer_cos], axis=1),
    )
    fwd_inner = (
        jnp.stack([inner_cos, -inner_sin], axis=1),
        jnp.stack([inner_sin, inner_cos], axis=1),
    )
    back_sign = jnp.array([-1.0, 1.0], jnp.float32)[:, None, None, None]
    fore_sign = jnp.array([1.0, -1.0], jnp.float32)[:, None, None, None]
    back_c = back_cos[None, :, :, None]
    back_s = back_sin[None, :, :, None] * back_sign
    fore_c = fore_cos[None, :, None, :]
    fore_s = fore_sin[None, :, None, :] * fore_sign

    node_ids = jnp.arange(node_dev, dtype=jnp.int32)
    turns = jnp.arange(groups, dtype=jnp.int32)
    recv_blocks = (node_index + turns) % groups
    send_blocks = (node_index - turns) % groups
    own_rows = lax.dynamic_slice_in_dim(terminals, node_index * node_dev, node_dev, 0)
    own_rot = own_rows.reshape(groups, capacity, 3)[recv_blocks].reshape(node_dev, 3)
    drain_hot = (own_rot[:, 0, None] == node_ids[None, :]).astype(jnp.float32)
    source_hot = (own_rot[:, 1, None] == node_ids[None, :]).astype(jnp.float32)
    incidence = drain_hot - source_hot
    arranged = terminals.reshape(groups, groups, capacity, 3)
    wanted = lax.dynamic_index_in_dim(arranged, node_index, axis=1, keepdims=False)
    wanted = wanted[send_blocks].reshape(node_dev, 3)
    gate_hot = (wanted[:, 2, None] == node_ids[None, :]).astype(jnp.float32)
    picks = jnp.concatenate([gate_hot, incidence, source_hot], axis=0)
    batch = (2, conductance.shape[1])
    picks_wide = jnp.broadcast_to(picks, batch + picks.shape)
    stamp_wide = jnp.broadcast_to(incidence.T, batch + incidence.T.shape)

    cond_blocks = conductance.reshape(
        conductance.shape[0], conductance.shape[1], groups, capacity, conductance.shape[3]
    )
    cond_rot = jnp.concatenate(
        [
            lax.dynamic_slice_in_dim(cond_blocks, recv_blocks[s], 1, axis=2)
            for s in range(groups)
        ],
        axis=2,
    ).reshape(conductance.shape)
    trans_g = cond_rot[0]
    output_g = cond_rot[1]

    block_size = conduct_blocks.shape[2]
    block_count = node_dev // block_size
    pattern_hot = (
        pattern[:, :, None] == jnp.arange(block_count, dtype=jnp.int32)[None, None, :]
    ).astype(jnp.float32)
    conduct_dense = contract(
        "bjc,bjrs->brcs", pattern_hot, conduct_blocks, lax.Precision.HIGHEST
    ).reshape(node_dev, node_dev)
    capacit_dense = contract(
        "bjc,bjrs->brcs", pattern_hot, capacit_blocks, lax.Precision.HIGHEST
    ).reshape(node_dev, node_dev)
    mna = jnp.stack([conduct_dense, capacit_dense])
    bin_index = bin_first[:, None] + outer_size * inner_range[None, :]
    signed = jnp.where(bin_index < samples // 2, bin_index, bin_index - samples)
    angular = (signed.astype(jnp.float32) * (2.0 * math.pi / samples))[:, None, :]

    def complex_dft(form, parts, mats):
        return contract(form, parts[0], mats[0], dft_precision) + contract(
            form, parts[1], mats[1], dft_precision
        )

    def product(vector):
        mixed = complex_dft("anb,bkm->kman", (vector[0], vector[1]), inv_inner)
        spread = lax.all_to_all(
            mixed * back_c + mixed[::-1] * back_s,
            "freq",
            split_axis=1,
            concat_axis=2,
            tiled=True,
        )
        signal = complex_dft("man,akl->kmnl", (spread[0], spread[1]), inv_outer)
        picked = contract("kmdn,kmnl->kmdl", picks_wide, signal, pick_precision)
        outgoing = picked[:, :, :node_dev]
        pieces = [outgoing[:, :, :capacity]]
        for s in range(1, groups):
            pieces.append(
                lax.ppermute(
                    outgoing[:, :, s * capacity : (s + 1) * capacity],
                    "node",
                    [(i, (i - s) % groups) for i in range(groups)],
                )
            )
        at_gate = jnp.concatenate(pieces, axis=2)
        drain_less_source = picked[:, :, node_dev : 2 * node_dev]
        at_source = picked[:, :, 2 * node_dev :]
        current = trans_g * (at_gate - at_source) + output_g * drain_less_source
        injected = contract("kmnd,kmdl->kmnl", stamp_wide, current, pick_precision)
        turned = complex_dft("mnl,lka->kmna", (injected[0], injected[1]), fwd_outer)
        collected = lax.all_to_all(
            turned * fore_c + turned[::-1] * fore_s,
            "freq",
            split_axis=3,
            concat_axis=1,
            tiled=True,
        )
        response = complex_dft("mna,mkb->kanb", (collected[0], collected[1]), fwd_inner)
        from_real = contract("jrs,asb->jarb", mna, vector[0], mna_precision)
        from_imag = contract("jrs,asb->jarb", mna, vector[1], mna_precision)
        return jnp.stack(
            [
                response[0] + from_real[0] - angular * from_imag[1],
                response[1] + from_imag[0] + angular * from_real[1],
            ]
        )

    return (product(first_vector), product(second_vector))


def solution(mesh):
    return jax.shard_map(
        body,
        mesh=mesh,
        in_specs=(
            P(None, "freq", "node", None),
            P(None, "freq", "node", None),
            P(None, "freq", "node", None),
            P(),
            P("node", None),
            P("node", None, None, None),
            P("node", None, None, None),
        ),
        out_specs=(P(None, "freq", "node", None), P(None, "freq", "node", None)),
        check_vma=False,
    )
```

```python
import math

import jax
import jax.numpy as jnp
from jax import lax
from jax.sharding import PartitionSpec as P

dft_precision = lax.Precision.HIGH
pick_precision = lax.Precision.HIGH
mna_precision = lax.Precision.HIGH


def contract(form, left, right, precision):
    return jnp.einsum(form, left, right, precision=precision)


def cos_sin(first, second, length):
    angle = (first[:, None] * second[None, :] % length).astype(jnp.float32) * (
        2.0 * math.pi / length
    )
    return (jnp.cos(angle), jnp.sin(angle))


def body(
    first_vector, second_vector, conductance, terminals, pattern, conduct_blocks, capacit_blocks
):
    freq_count = lax.axis_size("freq")
    groups = lax.axis_size("node")
    local_bins = first_vector.shape[1]
    node_dev = first_vector.shape[2]
    inner_size = first_vector.shape[3]
    outer_size = local_bins * freq_count
    samples = outer_size * inner_size
    local_steps = inner_size // freq_count
    capacity = node_dev // groups
    freq_index = lax.axis_index("freq")
    node_index = lax.axis_index("node")
    bin_first = freq_index * local_bins + jnp.arange(local_bins, dtype=jnp.int32)
    step_first = freq_index * local_steps + jnp.arange(local_steps, dtype=jnp.int32)
    inner_range = jnp.arange(inner_size, dtype=jnp.int32)
    outer_range = jnp.arange(outer_size, dtype=jnp.int32)
    inner_cos, inner_sin = cos_sin(inner_range, inner_range, inner_size)
    outer_cos, outer_sin = cos_sin(outer_range, outer_range, outer_size)
    back_cos, back_sin = cos_sin(inner_range, bin_first, samples)
    fore_cos, fore_sin = cos_sin(step_first, outer_range, samples)
    scale = 1.0 / samples
    inv_inner = (
        jnp.stack([inner_cos, inner_sin], axis=1),
        jnp.stack([-inner_sin, inner_cos], axis=1),
    )
    inv_outer = (
        jnp.stack([outer_cos, outer_sin], axis=1) * scale,
        jnp.stack([-outer_sin, outer_cos], axis=1) * scale,
    )
    fwd_outer = (
        jnp.stack([outer_cos, -outer_sin], axis=1),
        jnp.stack([outer_sin, outer_cos], axis=1),
    )
    fwd_inner = (
        jnp.stack([inner_cos, -inner_sin], axis=1),
        jnp.stack([inner_sin, inner_cos], axis=1),
    )
    back_sign = jnp.array([-1.0, 1.0], jnp.float32)[:, None, None, None]
    fore_sign = jnp.array([1.0, -1.0], jnp.float32)[:, None, None, None]
    back_cos, back_sin, fore_cos, fore_sin = lax.optimization_barrier(
        (back_cos, back_sin, fore_cos, fore_sin)
    )
    back_c = back_cos[None, :, :, None]
    back_s = back_sin[None, :, :, None] * back_sign
    fore_c = fore_cos[None, :, None, :]
    fore_s = fore_sin[None, :, None, :] * fore_sign

    node_ids = jnp.arange(node_dev, dtype=jnp.int32)
    turns = jnp.arange(groups, dtype=jnp.int32)
    recv_blocks = (node_index + turns) % groups
    send_blocks = (node_index - turns) % groups
    own_rows = lax.dynamic_slice_in_dim(terminals, node_index * node_dev, node_dev, 0)
    own_rot = own_rows.reshape(groups, capacity, 3)[recv_blocks].reshape(node_dev, 3)
    drain_hot = (own_rot[:, 0, None] == node_ids[None, :]).astype(jnp.float32)
    source_hot = (own_rot[:, 1, None] == node_ids[None, :]).astype(jnp.float32)
    incidence = drain_hot - source_hot
    arranged = terminals.reshape(groups, groups, capacity, 3)
    wanted = lax.dynamic_index_in_dim(arranged, node_index, axis=1, keepdims=False)
    wanted = wanted[send_blocks].reshape(node_dev, 3)
    gate_hot = (wanted[:, 2, None] == node_ids[None, :]).astype(jnp.float32)
    picks = jnp.concatenate([gate_hot, incidence, source_hot], axis=0)
    batch = (2, 2, conductance.shape[1])
    picks_wide = jnp.broadcast_to(picks, batch + picks.shape)
    stamp_wide = jnp.broadcast_to(incidence.T, batch + incidence.T.shape)

    cond_blocks = conductance.reshape(
        conductance.shape[0], conductance.shape[1], groups, capacity, conductance.shape[3]
    )
    cond_rot = jnp.concatenate(
        [
            lax.dynamic_slice_in_dim(cond_blocks, recv_blocks[s], 1, axis=2)
            for s in range(groups)
        ],
        axis=2,
    ).reshape(conductance.shape)
    trans_g = cond_rot[0]
    output_g = cond_rot[1]

    block_size = conduct_blocks.shape[2]
    block_count = node_dev // block_size
    pattern_hot = (
        pattern[:, :, None] == jnp.arange(block_count, dtype=jnp.int32)[None, None, :]
    ).astype(jnp.float32)
    conduct_dense = contract(
        "bjc,bjrs->brcs", pattern_hot, conduct_blocks, lax.Precision.HIGHEST
    ).reshape(node_dev, node_dev)
    capacit_dense = contract(
        "bjc,bjrs->brcs", pattern_hot, capacit_blocks, lax.Precision.HIGHEST
    ).reshape(node_dev, node_dev)
    mna = jnp.stack([conduct_dense, capacit_dense])
    bin_index = bin_first[:, None] + outer_size * inner_range[None, :]
    signed = jnp.where(bin_index < samples // 2, bin_index, bin_index - samples)
    angular = (signed.astype(jnp.float32) * (2.0 * math.pi / samples))[:, None, :]

    def complex_dft(form, parts, mats):
        return contract(form, parts[0], mats[0], dft_precision) + contract(
            form, parts[1], mats[1], dft_precision
        )

    def product(both):
        mixed = complex_dft("vanb,bkm->vkman", (both[:, 0], both[:, 1]), inv_inner)
        spread = lax.all_to_all(
            mixed * back_c + mixed[:, ::-1] * back_s,
            "freq",
            split_axis=2,
            concat_axis=3,
            tiled=True,
        )
        signal = complex_dft("vman,akl->vkmnl", (spread[:, 0], spread[:, 1]), inv_outer)
        picked = contract("vkmdn,vkmnl->vkmdl", picks_wide, signal, pick_precision)
        outgoing = picked[:, :, :, :node_dev]
        pieces = [outgoing[:, :, :, :capacity]]
        for s in range(1, groups):
            pieces.append(
                lax.ppermute(
                    outgoing[:, :, :, s * capacity : (s + 1) * capacity],
                    "node",
                    [(i, (i - s) % groups) for i in range(groups)],
                )
            )
        at_gate = jnp.concatenate(pieces, axis=3)
        drain_less_source = picked[:, :, :, node_dev : 2 * node_dev]
        at_source = picked[:, :, :, 2 * node_dev :]
        current = trans_g * (at_gate - at_source) + output_g * drain_less_source
        injected = contract("vkmnd,vkmdl->vkmnl", stamp_wide, current, pick_precision)
        turned = complex_dft("vmnl,lka->vkmna", (injected[:, 0], injected[:, 1]), fwd_outer)
        collected = lax.all_to_all(
            turned * fore_c + turned[:, ::-1] * fore_s,
            "freq",
            split_axis=4,
            concat_axis=2,
            tiled=True,
        )
        return complex_dft("vmna,mkb->vkanb", (collected[:, 0], collected[:, 1]), fwd_inner)

    def with_mna(vector, response):
        from_real = contract("jrs,asb->jarb", mna, vector[0], mna_precision)
        from_imag = contract("jrs,asb->jarb", mna, vector[1], mna_precision)
        return jnp.stack(
            [
                response[0] + from_real[0] - angular * from_imag[1],
                response[1] + from_imag[0] + angular * from_real[1],
            ]
        )

    responses = product(jnp.stack([first_vector, second_vector]))
    return (
        with_mna(first_vector, responses[0]),
        with_mna(second_vector, responses[1]),
    )


def solution(mesh):
    return jax.shard_map(
        body,
        mesh=mesh,
        in_specs=(
            P(None, "freq", "node", None),
            P(None, "freq", "node", None),
            P(None, "freq", "node", None),
            P(),
            P("node", None),
            P("node", None, None, None),
            P("node", None, None, None),
        ),
        out_specs=(P(None, "freq", "node", None), P(None, "freq", "node", None)),
        check_vma=False,
    )
```

```python
import math

import jax
import jax.numpy as jnp
from jax import lax
from jax.sharding import PartitionSpec as P


dft_precision = lax.Precision.HIGH
pick_precision = lax.Precision.HIGH
mna_precision = lax.Precision.HIGH


def contract(form, left, right, precision):
    return jnp.einsum(form, left, right, precision=precision)


def cos_sin(first, second, length):
    angle = (first[:, None] * second[None, :] % length).astype(jnp.float32) * (
        2.0 * math.pi / length
    )
    return (jnp.cos(angle), jnp.sin(angle))


def body(
    first_vector, second_vector, conductance, terminals, pattern, conduct_blocks, capacit_blocks
):
    freq_count = lax.axis_size("freq")
    groups = lax.axis_size("node")
    local_bins = first_vector.shape[1]
    node_dev = first_vector.shape[2]
    inner_size = first_vector.shape[3]
    outer_size = local_bins * freq_count
    samples = outer_size * inner_size
    local_steps = inner_size // freq_count
    capacity = node_dev // groups
    freq_index = lax.axis_index("freq")
    node_index = lax.axis_index("node")
    bin_first = freq_index * local_bins + jnp.arange(local_bins, dtype=jnp.int32)
    step_first = freq_index * local_steps + jnp.arange(local_steps, dtype=jnp.int32)
    inner_range = jnp.arange(inner_size, dtype=jnp.int32)
    outer_range = jnp.arange(outer_size, dtype=jnp.int32)
    inner_cos, inner_sin = cos_sin(inner_range, inner_range, inner_size)
    outer_cos, outer_sin = cos_sin(outer_range, outer_range, outer_size)
    back_cos, back_sin = cos_sin(inner_range, bin_first, samples)
    fore_cos, fore_sin = cos_sin(step_first, outer_range, samples)
    scale = 1.0 / samples
    inv_inner = (
        jnp.stack([inner_cos, inner_sin], axis=1),
        jnp.stack([-inner_sin, inner_cos], axis=1),
    )
    inv_outer = (
        jnp.stack([outer_cos, outer_sin], axis=1) * scale,
        jnp.stack([-outer_sin, outer_cos], axis=1) * scale,
    )
    fwd_outer = (
        jnp.stack([outer_cos, -outer_sin], axis=1),
        jnp.stack([outer_sin, outer_cos], axis=1),
    )
    fwd_inner = (
        jnp.stack([inner_cos, -inner_sin], axis=1),
        jnp.stack([inner_sin, inner_cos], axis=1),
    )
    back_sign = jnp.array([-1.0, 1.0], jnp.float32)[:, None, None, None]
    fore_sign = jnp.array([1.0, -1.0], jnp.float32)[:, None, None, None]
    back_cos, back_sin, fore_cos, fore_sin = lax.optimization_barrier(
        (back_cos, back_sin, fore_cos, fore_sin)
    )
    back_c = back_cos[None, :, :, None]
    back_s = back_sin[None, :, :, None] * back_sign
    fore_c = fore_cos[None, :, None, :]
    fore_s = fore_sin[None, :, None, :] * fore_sign

    node_ids = jnp.arange(node_dev, dtype=jnp.int32)
    turns = jnp.arange(groups, dtype=jnp.int32)
    recv_blocks = (node_index + turns) % groups
    send_blocks = (node_index - turns) % groups
    own_rows = lax.dynamic_slice_in_dim(terminals, node_index * node_dev, node_dev, 0)
    own_rot = own_rows.reshape(groups, capacity, 3)[recv_blocks].reshape(node_dev, 3)
    drain_hot = (own_rot[:, 0, None] == node_ids[None, :]).astype(jnp.float32)
    source_hot = (own_rot[:, 1, None] == node_ids[None, :]).astype(jnp.float32)
    incidence = drain_hot - source_hot
    arranged = terminals.reshape(groups, groups, capacity, 3)
    wanted = lax.dynamic_index_in_dim(arranged, node_index, axis=1, keepdims=False)
    wanted = wanted[send_blocks].reshape(node_dev, 3)
    gate_hot = (wanted[:, 2, None] == node_ids[None, :]).astype(jnp.float32)
    picks = jnp.concatenate([gate_hot, incidence, source_hot], axis=0)
    batch = (2, conductance.shape[1])
    picks_wide = jnp.broadcast_to(picks, batch + picks.shape)
    stamp_wide = jnp.broadcast_to(incidence.T, batch + incidence.T.shape)

    cond_blocks = conductance.reshape(
        conductance.shape[0], conductance.shape[1], groups, capacity, conductance.shape[3]
    )
    cond_rot = jnp.concatenate(
        [
            lax.dynamic_slice_in_dim(cond_blocks, recv_blocks[s], 1, axis=2)
            for s in range(groups)
        ],
        axis=2,
    ).reshape(conductance.shape)
    trans_g = cond_rot[0]
    output_g = cond_rot[1]

    block_size = conduct_blocks.shape[2]
    block_count = node_dev // block_size
    pattern_hot = (
        pattern[:, :, None] == jnp.arange(block_count, dtype=jnp.int32)[None, None, :]
    ).astype(jnp.float32)
    conduct_dense = contract(
        "bjc,bjrs->brcs", pattern_hot, conduct_blocks, lax.Precision.HIGHEST
    ).reshape(node_dev, node_dev)
    capacit_dense = contract(
        "bjc,bjrs->brcs", pattern_hot, capacit_blocks, lax.Precision.HIGHEST
    ).reshape(node_dev, node_dev)
    mna = jnp.stack([conduct_dense, capacit_dense])
    bin_index = bin_first[:, None] + outer_size * inner_range[None, :]
    signed = jnp.where(bin_index < samples // 2, bin_index, bin_index - samples)
    angular = (signed.astype(jnp.float32) * (2.0 * math.pi / samples))[:, None, :]

    def complex_dft(form, parts, mats):
        return contract(form, parts[0], mats[0], dft_precision) + contract(
            form, parts[1], mats[1], dft_precision
        )

    def inner(vector):
        mixed = complex_dft("anb,bkm->kman", (vector[0], vector[1]), inv_inner)
        return mixed * back_c + mixed[::-1] * back_s

    def inverse_exchange(twisted):
        return lax.all_to_all(twisted, "freq", split_axis=1, concat_axis=2, tiled=True)

    def middle(spread):
        signal = complex_dft("man,akl->kmnl", (spread[0], spread[1]), inv_outer)
        picked = contract("kmdn,kmnl->kmdl", picks_wide, signal, pick_precision)
        outgoing = picked[:, :, :node_dev]
        pieces = [outgoing[:, :, :capacity]]
        for s in range(1, groups):
            pieces.append(
                lax.ppermute(
                    outgoing[:, :, s * capacity : (s + 1) * capacity],
                    "node",
                    [(i, (i - s) % groups) for i in range(groups)],
                )
            )
        at_gate = jnp.concatenate(pieces, axis=2)
        drain_less_source = picked[:, :, node_dev : 2 * node_dev]
        at_source = picked[:, :, 2 * node_dev :]
        current = trans_g * (at_gate - at_source) + output_g * drain_less_source
        injected = contract("kmnd,kmdl->kmnl", stamp_wide, current, pick_precision)
        turned = complex_dft("mnl,lka->kmna", (injected[0], injected[1]), fwd_outer)
        return turned * fore_c + turned[::-1] * fore_s

    def forward_exchange(twisted):
        return lax.all_to_all(twisted, "freq", split_axis=3, concat_axis=1, tiled=True)

    def outer(vector, collected):
        response = complex_dft("mna,mkb->kanb", (collected[0], collected[1]), fwd_inner)
        from_real = contract("jrs,asb->jarb", mna, vector[0], mna_precision)
        from_imag = contract("jrs,asb->jarb", mna, vector[1], mna_precision)
        return jnp.stack(
            [
                response[0] + from_real[0] - angular * from_imag[1],
                response[1] + from_imag[0] + angular * from_real[1],
            ]
        )

    first_twisted = inner(first_vector)
    first_twisted, second_held = lax.optimization_barrier((first_twisted, second_vector))
    first_spread = inverse_exchange(first_twisted)
    second_twisted = inner(second_held)
    second_spread = inverse_exchange(second_twisted)
    first_turned = middle(first_spread)
    first_turned, second_spread = lax.optimization_barrier((first_turned, second_spread))
    first_collected = forward_exchange(first_turned)
    second_turned = middle(second_spread)
    second_collected = forward_exchange(second_turned)
    first_product = outer(first_vector, first_collected)
    second_product = outer(second_vector, second_collected)
    return (first_product, second_product)


def solution(mesh):
    return step(mesh)


def step(mesh):
    return jax.shard_map(
        body,
        mesh=mesh,
        in_specs=(
            P(None, "freq", "node", None),
            P(None, "freq", "node", None),
            P(None, "freq", "node", None),
            P(),
            P("node", None),
            P("node", None, None, None),
            P("node", None, None, None),
        ),
        out_specs=(P(None, "freq", "node", None), P(None, "freq", "node", None)),
        check_vma=False,
    )
```

```python
import math

import jax
import jax.numpy as jnp
from jax import lax
from jax.sharding import PartitionSpec as P


dft_precision = lax.Precision.HIGH
pick_precision = lax.Precision.HIGH
mna_precision = lax.Precision.HIGH


def contract(form, left, right, precision):
    return jnp.einsum(form, left, right, precision=precision)


def cos_sin(first, second, length):
    angle = (first[:, None] * second[None, :] % length).astype(jnp.float32) * (
        2.0 * math.pi / length
    )
    return (jnp.cos(angle), jnp.sin(angle))


def body(
    first_vector, second_vector, conductance, terminals, pattern, conduct_blocks, capacit_blocks
):
    freq_count = lax.axis_size("freq")
    groups = lax.axis_size("node")
    local_bins = first_vector.shape[1]
    node_dev = first_vector.shape[2]
    inner_size = first_vector.shape[3]
    outer_size = local_bins * freq_count
    samples = outer_size * inner_size
    local_steps = inner_size // freq_count
    capacity = node_dev // groups
    freq_index = lax.axis_index("freq")
    node_index = lax.axis_index("node")
    bin_first = freq_index * local_bins + jnp.arange(local_bins, dtype=jnp.int32)
    step_first = freq_index * local_steps + jnp.arange(local_steps, dtype=jnp.int32)
    inner_range = jnp.arange(inner_size, dtype=jnp.int32)
    outer_range = jnp.arange(outer_size, dtype=jnp.int32)
    inner_cos, inner_sin = cos_sin(inner_range, inner_range, inner_size)
    outer_cos, outer_sin = cos_sin(outer_range, outer_range, outer_size)
    back_cos, back_sin = cos_sin(inner_range, bin_first, samples)
    fore_cos, fore_sin = cos_sin(step_first, outer_range, samples)
    scale = 1.0 / samples
    inv_inner = (
        jnp.stack([inner_cos, inner_sin], axis=1),
        jnp.stack([-inner_sin, inner_cos], axis=1),
    )
    inv_outer = (
        jnp.stack([outer_cos, outer_sin], axis=1) * scale,
        jnp.stack([-outer_sin, outer_cos], axis=1) * scale,
    )
    fwd_outer = (
        jnp.stack([outer_cos, -outer_sin], axis=1),
        jnp.stack([outer_sin, outer_cos], axis=1),
    )
    fwd_inner = (
        jnp.stack([inner_cos, -inner_sin], axis=1),
        jnp.stack([inner_sin, inner_cos], axis=1),
    )
    back_sign = jnp.array([-1.0, 1.0], jnp.float32)[:, None, None, None]
    fore_sign = jnp.array([1.0, -1.0], jnp.float32)[:, None, None, None]
    back_cos, back_sin, fore_cos, fore_sin = lax.optimization_barrier(
        (back_cos, back_sin, fore_cos, fore_sin)
    )
    back_c = back_cos[None, :, :, None]
    back_s = back_sin[None, :, :, None] * back_sign
    fore_c = fore_cos[None, :, None, :]
    fore_s = fore_sin[None, :, None, :] * fore_sign

    node_ids = jnp.arange(node_dev, dtype=jnp.int32)
    turns = jnp.arange(groups, dtype=jnp.int32)
    recv_blocks = (node_index + turns) % groups
    send_blocks = (node_index - turns) % groups
    own_rows = lax.dynamic_slice_in_dim(terminals, node_index * node_dev, node_dev, 0)
    own_rot = own_rows.reshape(groups, capacity, 3)[recv_blocks].reshape(node_dev, 3)
    drain_hot = (own_rot[:, 0, None] == node_ids[None, :]).astype(jnp.float32)
    source_hot = (own_rot[:, 1, None] == node_ids[None, :]).astype(jnp.float32)
    incidence = drain_hot - source_hot
    arranged = terminals.reshape(groups, groups, capacity, 3)
    wanted = lax.dynamic_index_in_dim(arranged, node_index, axis=1, keepdims=False)
    wanted = wanted[send_blocks].reshape(node_dev, 3)
    gate_hot = (wanted[:, 2, None] == node_ids[None, :]).astype(jnp.float32)
    picks = jnp.concatenate([gate_hot, incidence, source_hot], axis=0)
    batch = (2, conductance.shape[1])
    picks_wide = jnp.broadcast_to(picks, batch + picks.shape)
    stamp_wide = jnp.broadcast_to(incidence.T, batch + incidence.T.shape)

    cond_blocks = conductance.reshape(
        conductance.shape[0], conductance.shape[1], groups, capacity, conductance.shape[3]
    )
    cond_rot = jnp.concatenate(
        [
            lax.dynamic_slice_in_dim(cond_blocks, recv_blocks[s], 1, axis=2)
            for s in range(groups)
        ],
        axis=2,
    ).reshape(conductance.shape)
    trans_g = cond_rot[0]
    output_g = cond_rot[1]

    block_size = conduct_blocks.shape[2]
    block_count = node_dev // block_size
    pattern_hot = (
        pattern[:, :, None] == jnp.arange(block_count, dtype=jnp.int32)[None, None, :]
    ).astype(jnp.float32)
    conduct_dense = contract(
        "bjc,bjrs->brcs", pattern_hot, conduct_blocks, lax.Precision.HIGHEST
    ).reshape(node_dev, node_dev)
    capacit_dense = contract(
        "bjc,bjrs->brcs", pattern_hot, capacit_blocks, lax.Precision.HIGHEST
    ).reshape(node_dev, node_dev)
    mna = jnp.stack([conduct_dense, capacit_dense])
    bin_index = bin_first[:, None] + outer_size * inner_range[None, :]
    signed = jnp.where(bin_index < samples // 2, bin_index, bin_index - samples)
    angular = (signed.astype(jnp.float32) * (2.0 * math.pi / samples))[:, None, :]

    def complex_dft(form, parts, mats):
        return contract(form, parts[0], mats[0], dft_precision) + contract(
            form, parts[1], mats[1], dft_precision
        )

    def inner(vector):
        mixed = complex_dft("anb,bkm->kman", (vector[0], vector[1]), inv_inner)
        return mixed * back_c + mixed[::-1] * back_s

    def inverse_exchange(twisted):
        return lax.all_to_all(twisted, "freq", split_axis=1, concat_axis=2, tiled=True)

    def gather(spread):
        signal = complex_dft("man,akl->kmnl", (spread[0], spread[1]), inv_outer)
        return contract("kmdn,kmnl->kmdl", picks_wide, signal, pick_precision)

    def exchange_gates(picked):
        outgoing = picked[:, :, :node_dev]
        pieces = [outgoing[:, :, :capacity]]
        for s in range(1, groups):
            pieces.append(
                lax.ppermute(
                    outgoing[:, :, s * capacity : (s + 1) * capacity],
                    "node",
                    [(i, (i - s) % groups) for i in range(groups)],
                )
            )
        return jnp.concatenate(pieces, axis=2)

    def finish(picked, at_gate):
        drain_less_source = picked[:, :, node_dev : 2 * node_dev]
        at_source = picked[:, :, 2 * node_dev :]
        current = trans_g * (at_gate - at_source) + output_g * drain_less_source
        injected = contract("kmnd,kmdl->kmnl", stamp_wide, current, pick_precision)
        turned = complex_dft("mnl,lka->kmna", (injected[0], injected[1]), fwd_outer)
        return turned * fore_c + turned[::-1] * fore_s

    def forward_exchange(twisted):
        return lax.all_to_all(twisted, "freq", split_axis=3, concat_axis=1, tiled=True)

    def outer(vector, collected):
        response = complex_dft("mna,mkb->kanb", (collected[0], collected[1]), fwd_inner)
        from_real = contract("jrs,asb->jarb", mna, vector[0], mna_precision)
        from_imag = contract("jrs,asb->jarb", mna, vector[1], mna_precision)
        return jnp.stack(
            [
                response[0] + from_real[0] - angular * from_imag[1],
                response[1] + from_imag[0] + angular * from_real[1],
            ]
        )

    first_twisted = inner(first_vector)
    first_twisted, second_held = lax.optimization_barrier((first_twisted, second_vector))
    first_spread = inverse_exchange(first_twisted)
    second_twisted = inner(second_held)
    second_spread = inverse_exchange(second_twisted)
    first_picked = gather(first_spread)
    first_picked, second_spread = lax.optimization_barrier((first_picked, second_spread))
    first_gates = exchange_gates(first_picked)
    second_picked = gather(second_spread)
    second_gates = exchange_gates(second_picked)
    first_turned = finish(first_picked, first_gates)
    first_turned, second_picked = lax.optimization_barrier((first_turned, second_picked))
    first_collected = forward_exchange(first_turned)
    second_turned = finish(second_picked, second_gates)
    second_collected = forward_exchange(second_turned)
    first_product = outer(first_vector, first_collected)
    second_product = outer(second_vector, second_collected)
    return (first_product, second_product)


def solution(mesh):
    return step(mesh)


def step(mesh):
    return jax.shard_map(
        body,
        mesh=mesh,
        in_specs=(
            P(None, "freq", "node", None),
            P(None, "freq", "node", None),
            P(None, "freq", "node", None),
            P(),
            P("node", None),
            P("node", None, None, None),
            P("node", None, None, None),
        ),
        out_specs=(P(None, "freq", "node", None), P(None, "freq", "node", None)),
        check_vma=False,
    )
```

```python
import math

import jax
import jax.numpy as jnp
from jax import lax
from jax.experimental.layout import Layout, with_layout_constraint
from jax.sharding import PartitionSpec as P


dft_precision = lax.Precision.HIGH
pick_precision = lax.Precision.HIGH
mna_precision = lax.Precision.HIGH


def contract(form, left, right, precision):
    return jnp.einsum(form, left, right, precision=precision)


def cos_sin(first, second, length):
    angle = (first[:, None] * second[None, :] % length).astype(jnp.float32) * (
        2.0 * math.pi / length
    )
    return (jnp.cos(angle), jnp.sin(angle))


def body(
    first_vector, second_vector, conductance, terminals, pattern, conduct_blocks, capacit_blocks
):
    freq_count = lax.axis_size("freq")
    groups = lax.axis_size("node")
    local_bins = first_vector.shape[1]
    node_dev = first_vector.shape[2]
    inner_size = first_vector.shape[3]
    outer_size = local_bins * freq_count
    samples = outer_size * inner_size
    local_steps = inner_size // freq_count
    capacity = node_dev // groups
    freq_index = lax.axis_index("freq")
    node_index = lax.axis_index("node")
    bin_first = freq_index * local_bins + jnp.arange(local_bins, dtype=jnp.int32)
    step_first = freq_index * local_steps + jnp.arange(local_steps, dtype=jnp.int32)
    inner_range = jnp.arange(inner_size, dtype=jnp.int32)
    outer_range = jnp.arange(outer_size, dtype=jnp.int32)
    inner_cos, inner_sin = cos_sin(inner_range, inner_range, inner_size)
    outer_cos, outer_sin = cos_sin(outer_range, outer_range, outer_size)
    back_cos, back_sin = cos_sin(inner_range, bin_first, samples)
    fore_cos, fore_sin = cos_sin(step_first, outer_range, samples)
    scale = 1.0 / samples
    inv_inner = (
        jnp.stack([inner_cos, inner_sin], axis=1),
        jnp.stack([-inner_sin, inner_cos], axis=1),
    )
    inv_outer = (
        jnp.stack([outer_cos, outer_sin], axis=1) * scale,
        jnp.stack([-outer_sin, outer_cos], axis=1) * scale,
    )
    fwd_outer = (
        jnp.stack([outer_cos, -outer_sin], axis=1),
        jnp.stack([outer_sin, outer_cos], axis=1),
    )
    fwd_inner = (
        jnp.stack([inner_cos, -inner_sin], axis=1),
        jnp.stack([inner_sin, inner_cos], axis=1),
    )
    back_sign = jnp.array([-1.0, 1.0], jnp.float32)[:, None, None, None]
    fore_sign = jnp.array([1.0, -1.0], jnp.float32)[:, None, None, None]
    back_cos, back_sin, fore_cos, fore_sin = lax.optimization_barrier(
        (back_cos, back_sin, fore_cos, fore_sin)
    )
    back_c = back_cos[None, :, :, None]
    back_s = back_sin[None, :, :, None] * back_sign
    fore_c = fore_cos[None, :, None, :]
    fore_s = fore_sin[None, :, None, :] * fore_sign

    node_ids = jnp.arange(node_dev, dtype=jnp.int32)
    turns = jnp.arange(groups, dtype=jnp.int32)
    recv_blocks = (node_index + turns) % groups
    send_blocks = (node_index - turns) % groups
    own_rows = lax.dynamic_slice_in_dim(terminals, node_index * node_dev, node_dev, 0)
    own_rot = own_rows.reshape(groups, capacity, 3)[recv_blocks].reshape(node_dev, 3)
    drain_hot = (own_rot[:, 0, None] == node_ids[None, :]).astype(jnp.float32)
    source_hot = (own_rot[:, 1, None] == node_ids[None, :]).astype(jnp.float32)
    incidence = drain_hot - source_hot
    arranged = terminals.reshape(groups, groups, capacity, 3)
    wanted = lax.dynamic_index_in_dim(arranged, node_index, axis=1, keepdims=False)
    wanted = wanted[send_blocks].reshape(node_dev, 3)
    gate_hot = (wanted[:, 2, None] == node_ids[None, :]).astype(jnp.float32)
    picks = jnp.concatenate([gate_hot, incidence, source_hot], axis=0)
    batch = (2, conductance.shape[1])
    picks_wide = jnp.broadcast_to(picks, batch + picks.shape)
    stamp_wide = jnp.broadcast_to(incidence.T, batch + incidence.T.shape)

    cond_blocks = conductance.reshape(
        conductance.shape[0], conductance.shape[1], groups, capacity, conductance.shape[3]
    )
    cond_rot = jnp.concatenate(
        [
            lax.dynamic_slice_in_dim(cond_blocks, recv_blocks[s], 1, axis=2)
            for s in range(groups)
        ],
        axis=2,
    ).reshape(conductance.shape)
    trans_g = cond_rot[0]
    output_g = cond_rot[1]

    block_size = conduct_blocks.shape[2]
    block_count = node_dev // block_size
    pattern_hot = (
        pattern[:, :, None] == jnp.arange(block_count, dtype=jnp.int32)[None, None, :]
    ).astype(jnp.float32)
    conduct_dense = contract(
        "bjc,bjrs->brcs", pattern_hot, conduct_blocks, lax.Precision.HIGHEST
    ).reshape(node_dev, node_dev)
    capacit_dense = contract(
        "bjc,bjrs->brcs", pattern_hot, capacit_blocks, lax.Precision.HIGHEST
    ).reshape(node_dev, node_dev)
    mna = jnp.stack([conduct_dense, capacit_dense])
    bin_index = bin_first[:, None] + outer_size * inner_range[None, :]
    signed = jnp.where(bin_index < samples // 2, bin_index, bin_index - samples)
    angular = (signed.astype(jnp.float32) * (2.0 * math.pi / samples))[:, None, :]

    def complex_dft(form, parts, mats):
        return contract(form, parts[0], mats[0], dft_precision) + contract(
            form, parts[1], mats[1], dft_precision
        )

    def inner(vector):
        mixed = complex_dft("anb,bkm->kman", (vector[0], vector[1]), inv_inner)
        return mixed * back_c + mixed[::-1] * back_s

    def inverse_exchange(twisted):
        return lax.all_to_all(twisted, "freq", split_axis=1, concat_axis=2, tiled=True)

    def gather(spread):
        signal = complex_dft("man,akl->kmnl", (spread[0], spread[1]), inv_outer)
        return contract("kmdn,kmnl->kmdl", picks_wide, signal, pick_precision)

    def exchange_gates(picked):
        outgoing = picked[:, :, :node_dev]
        pieces = [outgoing[:, :, :capacity]]
        for s in range(1, groups):
            pieces.append(
                lax.ppermute(
                    outgoing[:, :, s * capacity : (s + 1) * capacity],
                    "node",
                    [(i, (i - s) % groups) for i in range(groups)],
                )
            )
        return jnp.concatenate(pieces, axis=2)

    def finish(picked, at_gate):
        drain_less_source = picked[:, :, node_dev : 2 * node_dev]
        at_source = picked[:, :, 2 * node_dev :]
        current = trans_g * (at_gate - at_source) + output_g * drain_less_source
        injected = contract("kmnd,kmdl->kmnl", stamp_wide, current, pick_precision)
        turned = complex_dft("mnl,lka->kmna", (injected[0], injected[1]), fwd_outer)
        return turned * fore_c + turned[::-1] * fore_s

    def forward_exchange(twisted):
        return lax.all_to_all(twisted, "freq", split_axis=3, concat_axis=1, tiled=True)

    def outer(vector, collected):
        response = complex_dft("mna,mkb->kanb", (collected[0], collected[1]), fwd_inner)
        response = with_layout_constraint(response, Layout(major_to_minor=(0, 1, 2, 3)))
        from_real = contract("jrs,asb->jarb", mna, vector[0], mna_precision)
        from_imag = contract("jrs,asb->jarb", mna, vector[1], mna_precision)
        return jnp.stack(
            [
                response[0] + from_real[0] - angular * from_imag[1],
                response[1] + from_imag[0] + angular * from_real[1],
            ]
        )

    first_twisted = inner(first_vector)
    first_twisted, second_held = lax.optimization_barrier((first_twisted, second_vector))
    first_spread = inverse_exchange(first_twisted)
    second_twisted = inner(second_held)
    second_spread = inverse_exchange(second_twisted)
    first_picked = gather(first_spread)
    first_gates = exchange_gates(first_picked)
    first_gates, second_spread = lax.optimization_barrier((first_gates, second_spread))
    second_picked = gather(second_spread)
    second_gates = exchange_gates(second_picked)
    first_turned = finish(first_picked, first_gates)
    first_turned, second_picked = lax.optimization_barrier((first_turned, second_picked))
    first_collected = forward_exchange(first_turned)
    second_turned = finish(second_picked, second_gates)
    second_collected = forward_exchange(second_turned)
    first_product = outer(first_vector, first_collected)
    first_product, second_collected = lax.optimization_barrier((first_product, second_collected))
    second_product = outer(second_vector, second_collected)
    return (first_product, second_product)


def solution(mesh):
    return step(mesh)


def step(mesh):
    return jax.shard_map(
        body,
        mesh=mesh,
        in_specs=(
            P(None, "freq", "node", None),
            P(None, "freq", "node", None),
            P(None, "freq", "node", None),
            P(),
            P("node", None),
            P("node", None, None, None),
            P("node", None, None, None),
        ),
        out_specs=(P(None, "freq", "node", None), P(None, "freq", "node", None)),
        check_vma=False,
    )
```

```python
import math

import jax
import jax.numpy as jnp
from jax import lax
from jax.experimental.layout import Layout, with_layout_constraint
from jax.sharding import PartitionSpec as P


dft_precision = lax.Precision.HIGH
mna_precision = lax.Precision.HIGH


def contract(form, left, right, precision):
    return jnp.einsum(form, left, right, precision=precision)


def cos_sin(first, second, length):
    angle = (first[:, None] * second[None, :] % length).astype(jnp.float32) * (
        2.0 * math.pi / length
    )
    return (jnp.cos(angle), jnp.sin(angle))


def body(
    first_vector, second_vector, conductance, terminals, pattern, conduct_blocks, capacit_blocks
):
    freq_count = lax.axis_size("freq")
    groups = lax.axis_size("node")
    local_bins = first_vector.shape[1]
    node_dev = first_vector.shape[2]
    inner_size = first_vector.shape[3]
    outer_size = local_bins * freq_count
    samples = outer_size * inner_size
    local_steps = inner_size // freq_count
    capacity = node_dev // groups
    freq_index = lax.axis_index("freq")
    node_index = lax.axis_index("node")
    bin_first = freq_index * local_bins + jnp.arange(local_bins, dtype=jnp.int32)
    step_first = freq_index * local_steps + jnp.arange(local_steps, dtype=jnp.int32)
    inner_range = jnp.arange(inner_size, dtype=jnp.int32)
    outer_range = jnp.arange(outer_size, dtype=jnp.int32)
    inner_cos, inner_sin = cos_sin(inner_range, inner_range, inner_size)
    outer_cos, outer_sin = cos_sin(outer_range, outer_range, outer_size)
    back_cos, back_sin = cos_sin(inner_range, bin_first, samples)
    fore_cos, fore_sin = cos_sin(step_first, outer_range, samples)
    scale = 1.0 / samples
    inv_inner = (
        jnp.stack([inner_cos, inner_sin], axis=1),
        jnp.stack([-inner_sin, inner_cos], axis=1),
    )
    inv_outer = (
        jnp.stack([outer_cos, outer_sin], axis=1) * scale,
        jnp.stack([-outer_sin, outer_cos], axis=1) * scale,
    )
    fwd_outer = (
        jnp.stack([outer_cos, -outer_sin], axis=1),
        jnp.stack([outer_sin, outer_cos], axis=1),
    )
    fwd_inner = (
        jnp.stack([inner_cos, -inner_sin], axis=1),
        jnp.stack([inner_sin, inner_cos], axis=1),
    )
    back_sign = jnp.array([-1.0, 1.0], jnp.float32)[:, None, None, None]
    fore_sign = jnp.array([1.0, -1.0], jnp.float32)[:, None, None, None]
    back_cos, back_sin, fore_cos, fore_sin = lax.optimization_barrier(
        (back_cos, back_sin, fore_cos, fore_sin)
    )
    back_c = back_cos[None, :, :, None]
    back_s = back_sin[None, :, :, None] * back_sign
    fore_c = fore_cos[None, :, None, :]
    fore_s = fore_sin[None, :, None, :] * fore_sign

    node_ids = jnp.arange(node_dev, dtype=jnp.int32)
    turns = jnp.arange(groups, dtype=jnp.int32)
    recv_blocks = (node_index + turns) % groups
    send_blocks = (node_index - turns) % groups
    own_rows = lax.dynamic_slice_in_dim(terminals, node_index * node_dev, node_dev, 0)
    own_rot = own_rows.reshape(groups, capacity, 3)[recv_blocks].reshape(node_dev, 3)
    drain_hot = (own_rot[:, 0, None] == node_ids[None, :]).astype(jnp.float32)
    source_hot = (own_rot[:, 1, None] == node_ids[None, :]).astype(jnp.float32)
    incidence = drain_hot - source_hot
    arranged = terminals.reshape(groups, groups, capacity, 3)
    wanted = lax.dynamic_index_in_dim(arranged, node_index, axis=1, keepdims=False)
    wanted = wanted[send_blocks].reshape(node_dev, 3)
    gate_hot = (wanted[:, 2, None] == node_ids[None, :]).astype(jnp.float32)
    local_picks = jnp.concatenate([incidence, source_hot], axis=0)
    batch = (2, conductance.shape[1])
    gate_wide = jnp.broadcast_to(gate_hot, batch + gate_hot.shape)
    local_wide = jnp.broadcast_to(local_picks, batch + local_picks.shape)
    stamp_wide = jnp.broadcast_to(incidence.T, batch + incidence.T.shape)

    cond_blocks = conductance.reshape(
        conductance.shape[0], conductance.shape[1], groups, capacity, conductance.shape[3]
    )
    cond_rot = jnp.concatenate(
        [
            lax.dynamic_slice_in_dim(cond_blocks, recv_blocks[s], 1, axis=2)
            for s in range(groups)
        ],
        axis=2,
    ).reshape(conductance.shape)
    trans_g = cond_rot[0]
    output_g = cond_rot[1]

    block_size = conduct_blocks.shape[2]
    block_count = node_dev // block_size
    pattern_hot = (
        pattern[:, :, None] == jnp.arange(block_count, dtype=jnp.int32)[None, None, :]
    ).astype(jnp.float32)
    conduct_dense = contract(
        "bjc,bjrs->brcs", pattern_hot, conduct_blocks, lax.Precision.HIGHEST
    ).reshape(node_dev, node_dev)
    capacit_dense = contract(
        "bjc,bjrs->brcs", pattern_hot, capacit_blocks, lax.Precision.HIGHEST
    ).reshape(node_dev, node_dev)
    mna = jnp.stack([conduct_dense, capacit_dense])
    bin_index = bin_first[:, None] + outer_size * inner_range[None, :]
    signed = jnp.where(bin_index < samples // 2, bin_index, bin_index - samples)
    angular = (signed.astype(jnp.float32) * (2.0 * math.pi / samples))[:, None, :]

    def select(form, hot, values):
        return contract(form, hot, values, lax.Precision.HIGH)

    def complex_dft(form, parts, mats):
        return contract(form, parts[0], mats[0], dft_precision) + contract(
            form, parts[1], mats[1], dft_precision
        )

    def inner(vector):
        mixed = complex_dft("anb,bkm->kman", (vector[0], vector[1]), inv_inner)
        return mixed * back_c + mixed[::-1] * back_s

    def inverse_exchange(twisted):
        return lax.all_to_all(twisted, "freq", split_axis=1, concat_axis=2, tiled=True)

    def gather(spread):
        signal = complex_dft("man,akl->kmnl", (spread[0], spread[1]), inv_outer)
        return signal, select("kmdn,kmnl->kmdl", gate_wide, signal)

    def exchange_gates(outgoing):
        pieces = [outgoing[:, :, :capacity]]
        for s in range(1, groups):
            pieces.append(
                lax.ppermute(
                    outgoing[:, :, s * capacity : (s + 1) * capacity],
                    "node",
                    [(i, (i - s) % groups) for i in range(groups)],
                )
            )
        return jnp.concatenate(pieces, axis=2)

    def finish(signal, at_gate):
        picked = select("kmdn,kmnl->kmdl", local_wide, signal)
        drain_less_source = picked[:, :, :node_dev]
        at_source = picked[:, :, node_dev:]
        current = trans_g * (at_gate - at_source) + output_g * drain_less_source
        injected = select("kmnd,kmdl->kmnl", stamp_wide, current)
        turned = complex_dft("mnl,lka->kmna", (injected[0], injected[1]), fwd_outer)
        return with_layout_constraint(
            turned * fore_c + turned[::-1] * fore_s, Layout(major_to_minor=(3, 0, 1, 2))
        )

    def forward_exchange(twisted):
        return lax.all_to_all(twisted, "freq", split_axis=3, concat_axis=1, tiled=True)

    def outer(vector, collected):
        response = complex_dft("mna,mkb->kanb", (collected[0], collected[1]), fwd_inner)
        response = with_layout_constraint(response, Layout(major_to_minor=(0, 1, 2, 3)))
        from_real = contract("jrs,asb->jarb", mna, vector[0], mna_precision)
        from_imag = contract("jrs,asb->jarb", mna, vector[1], mna_precision)
        return jnp.stack(
            [
                response[0] + from_real[0] - angular * from_imag[1],
                response[1] + from_imag[0] + angular * from_real[1],
            ]
        )

    first_twisted = inner(first_vector)
    first_twisted, second_held = lax.optimization_barrier((first_twisted, second_vector))
    first_spread = inverse_exchange(first_twisted)
    second_twisted = inner(second_held)
    second_spread = inverse_exchange(second_twisted)
    first_signal, first_outgoing = gather(first_spread)
    first_gates = exchange_gates(first_outgoing)
    first_gates, second_spread = lax.optimization_barrier((first_gates, second_spread))
    second_signal, second_outgoing = gather(second_spread)
    second_gates = exchange_gates(second_outgoing)
    first_turned = finish(first_signal, first_gates)
    first_turned, second_signal = lax.optimization_barrier((first_turned, second_signal))
    first_collected = forward_exchange(first_turned)
    second_turned = finish(second_signal, second_gates)
    second_collected = forward_exchange(second_turned)
    first_product = outer(first_vector, first_collected)
    first_product, second_collected = lax.optimization_barrier((first_product, second_collected))
    second_product = outer(second_vector, second_collected)
    return (first_product, second_product)


def solution(mesh):
    return step(mesh)


def step(mesh):
    return jax.shard_map(
        body,
        mesh=mesh,
        in_specs=(
            P(None, "freq", "node", None),
            P(None, "freq", "node", None),
            P(None, "freq", "node", None),
            P(),
            P("node", None),
            P("node", None, None, None),
            P("node", None, None, None),
        ),
        out_specs=(P(None, "freq", "node", None), P(None, "freq", "node", None)),
        check_vma=False,
    )
```

```python
import math

import jax
import jax.numpy as jnp
from jax import lax
from jax.experimental.layout import Layout, with_layout_constraint
from jax.sharding import PartitionSpec as P


dft_precision = lax.Precision.HIGH
mna_precision = lax.Precision.HIGH


def contract(form, left, right, precision):
    return jnp.einsum(form, left, right, precision=precision)


def cos_sin(first, second, length):
    angle = (first[:, None] * second[None, :] % length).astype(jnp.float32) * (
        2.0 * math.pi / length
    )
    return (jnp.cos(angle), jnp.sin(angle))


def body(
    first_vector, second_vector, conductance, terminals, pattern, conduct_blocks, capacit_blocks
):
    freq_count = lax.axis_size("freq")
    groups = lax.axis_size("node")
    local_bins = first_vector.shape[1]
    node_dev = first_vector.shape[2]
    inner_size = first_vector.shape[3]
    outer_size = local_bins * freq_count
    samples = outer_size * inner_size
    local_steps = inner_size // freq_count
    capacity = node_dev // groups
    freq_index = lax.axis_index("freq")
    node_index = lax.axis_index("node")
    bin_first = freq_index * local_bins + jnp.arange(local_bins, dtype=jnp.int32)
    step_first = freq_index * local_steps + jnp.arange(local_steps, dtype=jnp.int32)
    inner_range = jnp.arange(inner_size, dtype=jnp.int32)
    outer_range = jnp.arange(outer_size, dtype=jnp.int32)
    inner_cos, inner_sin = cos_sin(inner_range, inner_range, inner_size)
    outer_cos, outer_sin = cos_sin(outer_range, outer_range, outer_size)
    back_cos, back_sin = cos_sin(inner_range, bin_first, samples)
    fore_cos, fore_sin = cos_sin(step_first, outer_range, samples)
    scale = 1.0 / samples
    inv_inner = (
        jnp.stack([inner_cos, inner_sin], axis=1),
        jnp.stack([-inner_sin, inner_cos], axis=1),
    )
    inv_outer = (
        jnp.stack([outer_cos, outer_sin], axis=1) * scale,
        jnp.stack([-outer_sin, outer_cos], axis=1) * scale,
    )
    fwd_outer = (
        jnp.stack([outer_cos, -outer_sin], axis=1),
        jnp.stack([outer_sin, outer_cos], axis=1),
    )
    fwd_inner = (
        jnp.stack([inner_cos, -inner_sin], axis=1),
        jnp.stack([inner_sin, inner_cos], axis=1),
    )
    back_sign = jnp.array([-1.0, 1.0], jnp.float32)[:, None, None, None]
    fore_sign = jnp.array([1.0, -1.0], jnp.float32)[:, None, None, None]
    back_cos, back_sin, fore_cos, fore_sin = lax.optimization_barrier(
        (back_cos, back_sin, fore_cos, fore_sin)
    )
    back_c = back_cos[None, :, :, None]
    back_s = back_sin[None, :, :, None] * back_sign
    fore_c = fore_cos[None, :, None, :]
    fore_s = fore_sin[None, :, None, :] * fore_sign

    node_ids = jnp.arange(node_dev, dtype=jnp.int32)
    turns = jnp.arange(groups, dtype=jnp.int32)
    recv_blocks = (node_index + turns) % groups
    send_blocks = (node_index - turns) % groups
    own_rows = lax.dynamic_slice_in_dim(terminals, node_index * node_dev, node_dev, 0)
    own_rot = own_rows.reshape(groups, capacity, 3)[recv_blocks].reshape(node_dev, 3)
    drain_hot = (own_rot[:, 0, None] == node_ids[None, :]).astype(jnp.float32)
    source_hot = (own_rot[:, 1, None] == node_ids[None, :]).astype(jnp.float32)
    incidence = drain_hot - source_hot
    arranged = terminals.reshape(groups, groups, capacity, 3)
    wanted = lax.dynamic_index_in_dim(arranged, node_index, axis=1, keepdims=False)
    wanted = wanted[send_blocks].reshape(node_dev, 3)
    gate_hot = (wanted[:, 2, None] == node_ids[None, :]).astype(jnp.float32)
    local_picks = jnp.concatenate([incidence, source_hot], axis=0)
    batch = (2, conductance.shape[1])
    gate_wide = jnp.broadcast_to(gate_hot, batch + gate_hot.shape)
    local_wide = jnp.broadcast_to(local_picks, batch + local_picks.shape)
    stamp_wide = jnp.broadcast_to(incidence.T, batch + incidence.T.shape)

    cond_blocks = conductance.reshape(
        conductance.shape[0], conductance.shape[1], groups, capacity, conductance.shape[3]
    )
    cond_rot = jnp.concatenate(
        [
            lax.dynamic_slice_in_dim(cond_blocks, recv_blocks[s], 1, axis=2)
            for s in range(groups)
        ],
        axis=2,
    ).reshape(conductance.shape)
    trans_g = cond_rot[0]
    output_g = cond_rot[1]

    block_size = conduct_blocks.shape[2]
    block_count = node_dev // block_size
    pattern_hot = (
        pattern[:, :, None] == jnp.arange(block_count, dtype=jnp.int32)[None, None, :]
    ).astype(jnp.float32)
    conduct_dense = contract(
        "bjc,bjrs->brcs", pattern_hot, conduct_blocks, lax.Precision.HIGHEST
    ).reshape(node_dev, node_dev)
    capacit_dense = contract(
        "bjc,bjrs->brcs", pattern_hot, capacit_blocks, lax.Precision.HIGHEST
    ).reshape(node_dev, node_dev)
    mna = jnp.stack([conduct_dense, capacit_dense])
    bin_index = bin_first[:, None] + outer_size * inner_range[None, :]
    signed = jnp.where(bin_index < samples // 2, bin_index, bin_index - samples)
    angular = (signed.astype(jnp.float32) * (2.0 * math.pi / samples))[:, None, :]

    def select(form, hot, values):
        return contract(form, hot, values, lax.Precision.HIGH)

    def complex_dft(form, parts, mats):
        return contract(form, parts[0], mats[0], dft_precision) + contract(
            form, parts[1], mats[1], dft_precision
        )

    def inner(vector):
        mixed = complex_dft("anb,bkm->kman", (vector[0], vector[1]), inv_inner)
        return mixed * back_c + mixed[::-1] * back_s

    def inverse_exchange(twisted):
        return lax.all_to_all(twisted, "freq", split_axis=1, concat_axis=2, tiled=True)

    def gather(spread):
        signal = complex_dft("man,akl->kmnl", (spread[0], spread[1]), inv_outer)
        return signal, select("kmdn,kmnl->kmdl", gate_wide, signal)

    def shift(x, s):
        return lax.ppermute(x, "node", [(i, (i - s) % groups) for i in range(groups)])

    def exchange_gates(outgoing):
        pieces = [outgoing[:, :, :capacity]]
        for s in range(1, groups):
            chunk = outgoing[:, :, s * capacity : (s + 1) * capacity]
            if 2 * s == groups:
                half = chunk.shape[1] // 2
                down = shift(shift(chunk[:, :half], 1), 1)
                up = shift(shift(chunk[:, half:], -1), -1)
                pieces.append(jnp.concatenate([down, up], axis=1))
            else:
                pieces.append(shift(chunk, s))
        return jnp.concatenate(pieces, axis=2)

    def finish(signal, at_gate):
        picked = select("kmdn,kmnl->kmdl", local_wide, signal)
        drain_less_source = picked[:, :, :node_dev]
        at_source = picked[:, :, node_dev:]
        current = trans_g * (at_gate - at_source) + output_g * drain_less_source
        injected = select("kmnd,kmdl->kmnl", stamp_wide, current)
        turned = complex_dft("mnl,lka->kmna", (injected[0], injected[1]), fwd_outer)
        return turned * fore_c + turned[::-1] * fore_s

    def forward_exchange(twisted):
        return lax.all_to_all(twisted, "freq", split_axis=3, concat_axis=1, tiled=True)

    def outer(vector, collected):
        response = complex_dft("mna,mkb->kanb", (collected[0], collected[1]), fwd_inner)
        response = with_layout_constraint(response, Layout(major_to_minor=(0, 1, 2, 3)))
        from_real = contract("jrs,asb->jarb", mna, vector[0], mna_precision)
        from_imag = contract("jrs,asb->jarb", mna, vector[1], mna_precision)
        return jnp.stack(
            [
                response[0] + from_real[0] - angular * from_imag[1],
                response[1] + from_imag[0] + angular * from_real[1],
            ]
        )

    first_twisted = inner(first_vector)
    first_twisted, second_held = lax.optimization_barrier((first_twisted, second_vector))
    first_spread = inverse_exchange(first_twisted)
    second_twisted = inner(second_held)
    second_spread = inverse_exchange(second_twisted)
    first_signal, first_outgoing = gather(first_spread)
    first_gates = exchange_gates(first_outgoing)
    first_gates, second_spread = lax.optimization_barrier((first_gates, second_spread))
    second_signal, second_outgoing = gather(second_spread)
    second_gates = exchange_gates(second_outgoing)
    first_turned = finish(first_signal, first_gates)
    first_turned, second_signal = lax.optimization_barrier((first_turned, second_signal))
    first_collected = forward_exchange(first_turned)
    second_turned = finish(second_signal, second_gates)
    second_collected = forward_exchange(second_turned)
    first_product = outer(first_vector, first_collected)
    first_product, second_collected = lax.optimization_barrier((first_product, second_collected))
    second_product = outer(second_vector, second_collected)
    return (first_product, second_product)


def solution(mesh):
    return step(mesh)


def step(mesh):
    return jax.shard_map(
        body,
        mesh=mesh,
        in_specs=(
            P(None, "freq", "node", None),
            P(None, "freq", "node", None),
            P(None, "freq", "node", None),
            P(),
            P("node", None),
            P("node", None, None, None),
            P("node", None, None, None),
        ),
        out_specs=(P(None, "freq", "node", None), P(None, "freq", "node", None)),
        check_vma=False,
    )
```

```python
import math

import jax
import jax.numpy as jnp
from jax import lax
from jax.experimental.layout import Layout, with_layout_constraint
from jax.sharding import PartitionSpec as P


dft_precision = lax.Precision.HIGH
mna_precision = lax.Precision.HIGH


def contract(form, left, right, precision):
    return jnp.einsum(form, left, right, precision=precision)


def cos_sin(first, second, length):
    angle = (first[:, None] * second[None, :] % length).astype(jnp.float32) * (
        2.0 * math.pi / length
    )
    return (jnp.cos(angle), jnp.sin(angle))


def body(
    first_vector, second_vector, conductance, terminals, pattern, conduct_blocks, capacit_blocks
):
    freq_count = lax.axis_size("freq")
    groups = lax.axis_size("node")
    local_bins = first_vector.shape[1]
    node_dev = first_vector.shape[2]
    inner_size = first_vector.shape[3]
    outer_size = local_bins * freq_count
    samples = outer_size * inner_size
    local_steps = inner_size // freq_count
    capacity = node_dev // groups
    freq_index = lax.axis_index("freq")
    node_index = lax.axis_index("node")
    bin_first = freq_index * local_bins + jnp.arange(local_bins, dtype=jnp.int32)
    step_first = freq_index * local_steps + jnp.arange(local_steps, dtype=jnp.int32)
    inner_range = jnp.arange(inner_size, dtype=jnp.int32)
    outer_range = jnp.arange(outer_size, dtype=jnp.int32)
    inner_cos, inner_sin = cos_sin(inner_range, inner_range, inner_size)
    outer_cos, outer_sin = cos_sin(outer_range, outer_range, outer_size)
    back_cos, back_sin = cos_sin(inner_range, bin_first, samples)
    fore_cos, fore_sin = cos_sin(step_first, outer_range, samples)
    scale = 1.0 / samples
    inv_inner = (
        jnp.stack([inner_cos, inner_sin], axis=1),
        jnp.stack([-inner_sin, inner_cos], axis=1),
    )
    inv_outer = (
        jnp.stack([outer_cos, outer_sin], axis=1) * scale,
        jnp.stack([-outer_sin, outer_cos], axis=1) * scale,
    )
    fwd_outer = (
        jnp.stack([outer_cos, -outer_sin], axis=1),
        jnp.stack([outer_sin, outer_cos], axis=1),
    )
    fwd_inner = (
        jnp.stack([inner_cos, -inner_sin], axis=1),
        jnp.stack([inner_sin, inner_cos], axis=1),
    )
    back_sign = jnp.array([-1.0, 1.0], jnp.float32)[:, None, None, None]
    fore_sign = jnp.array([1.0, -1.0], jnp.float32)[:, None, None, None]
    back_cos, back_sin, fore_cos, fore_sin = lax.optimization_barrier(
        (back_cos, back_sin, fore_cos, fore_sin)
    )
    back_c = back_cos[None, :, :, None]
    back_s = back_sin[None, :, :, None] * back_sign
    fore_c = fore_cos[None, :, None, :]
    fore_s = fore_sin[None, :, None, :] * fore_sign

    node_ids = jnp.arange(node_dev, dtype=jnp.int32)
    turns = jnp.arange(groups, dtype=jnp.int32)
    recv_blocks = (node_index + turns) % groups
    send_blocks = (node_index - turns) % groups
    own_rows = lax.dynamic_slice_in_dim(terminals, node_index * node_dev, node_dev, 0)
    own_rot = own_rows.reshape(groups, capacity, 3)[recv_blocks].reshape(node_dev, 3)
    drain_hot = (own_rot[:, 0, None] == node_ids[None, :]).astype(jnp.float32)
    source_hot = (own_rot[:, 1, None] == node_ids[None, :]).astype(jnp.float32)
    incidence = drain_hot - source_hot
    arranged = terminals.reshape(groups, groups, capacity, 3)
    wanted = lax.dynamic_index_in_dim(arranged, node_index, axis=1, keepdims=False)
    wanted = wanted[send_blocks].reshape(node_dev, 3)
    gate_hot = (wanted[:, 2, None] == node_ids[None, :]).astype(jnp.float32)
    local_picks = jnp.concatenate([incidence, source_hot], axis=0)
    batch = (2, conductance.shape[1])
    gate_wide = jnp.broadcast_to(gate_hot, batch + gate_hot.shape)
    local_wide = jnp.broadcast_to(local_picks, batch + local_picks.shape)
    stamp_wide = jnp.broadcast_to(incidence.T, batch + incidence.T.shape)

    cond_blocks = conductance.reshape(
        conductance.shape[0], conductance.shape[1], groups, capacity, conductance.shape[3]
    )
    cond_rot = jnp.concatenate(
        [
            lax.dynamic_slice_in_dim(cond_blocks, recv_blocks[s], 1, axis=2)
            for s in range(groups)
        ],
        axis=2,
    ).reshape(conductance.shape)
    trans_g = cond_rot[0]
    output_g = cond_rot[1]

    block_size = conduct_blocks.shape[2]
    block_count = node_dev // block_size
    pattern_hot = (
        pattern[:, :, None] == jnp.arange(block_count, dtype=jnp.int32)[None, None, :]
    ).astype(jnp.float32)
    conduct_dense = contract(
        "bjc,bjrs->brcs", pattern_hot, conduct_blocks, lax.Precision.HIGHEST
    ).reshape(node_dev, node_dev)
    capacit_dense = contract(
        "bjc,bjrs->brcs", pattern_hot, capacit_blocks, lax.Precision.HIGHEST
    ).reshape(node_dev, node_dev)
    mna = jnp.stack([conduct_dense, capacit_dense])
    bin_index = bin_first[:, None] + outer_size * inner_range[None, :]
    signed = jnp.where(bin_index < samples // 2, bin_index, bin_index - samples)
    angular = (signed.astype(jnp.float32) * (2.0 * math.pi / samples))[:, None, :]

    def select(form, hot, values):
        return contract(form, hot, values, lax.Precision.HIGH)

    def complex_dft(form, parts, mats):
        return contract(form, parts[0], mats[0], dft_precision) + contract(
            form, parts[1], mats[1], dft_precision
        )

    def inner(vector):
        mixed = complex_dft("anb,bkm->kman", (vector[0], vector[1]), inv_inner)
        return mixed * back_c + mixed[::-1] * back_s

    def inverse_exchange(twisted):
        return lax.all_to_all(twisted, "freq", split_axis=1, concat_axis=2, tiled=True)

    def gather(spread):
        signal = complex_dft("man,akl->kmnl", (spread[0], spread[1]), inv_outer)
        return signal, select("kmdn,kmnl->kmdl", gate_wide, signal)

    def exchange_gates(outgoing):
        pieces = [outgoing[:, :, :capacity]]
        for s in range(1, groups):
            pieces.append(
                lax.ppermute(
                    outgoing[:, :, s * capacity : (s + 1) * capacity],
                    "node",
                    [(i, (i - s) % groups) for i in range(groups)],
                )
            )
        return jnp.concatenate(pieces, axis=2)

    def finish(signal, at_gate):
        picked = select("kmdn,kmnl->kmdl", local_wide, signal)
        drain_less_source = picked[:, :, :node_dev]
        at_source = picked[:, :, node_dev:]
        current = trans_g * (at_gate - at_source) + output_g * drain_less_source
        injected = select("kmnd,kmdl->kmnl", stamp_wide, current)
        turned = complex_dft("mnl,lka->kmna", (injected[0], injected[1]), fwd_outer)
        return turned * fore_c + turned[::-1] * fore_s

    def forward_exchange(twisted):
        return lax.all_to_all(twisted, "freq", split_axis=3, concat_axis=1, tiled=True)

    def outer(vector, collected, row_major):
        response = complex_dft("mna,mkb->kanb", (collected[0], collected[1]), fwd_inner)
        if row_major:
            response = with_layout_constraint(response, Layout(major_to_minor=(0, 1, 2, 3)))
        from_real = contract("jrs,asb->jarb", mna, vector[0], mna_precision)
        from_imag = contract("jrs,asb->jarb", mna, vector[1], mna_precision)
        return jnp.stack(
            [
                response[0] + from_real[0] - angular * from_imag[1],
                response[1] + from_imag[0] + angular * from_real[1],
            ]
        )

    first_twisted = inner(first_vector)
    first_twisted, second_held = lax.optimization_barrier((first_twisted, second_vector))
    first_spread = inverse_exchange(first_twisted)
    second_twisted = inner(second_held)
    second_spread = inverse_exchange(second_twisted)
    first_signal, first_outgoing = gather(first_spread)
    first_gates = exchange_gates(first_outgoing)
    first_gates, second_spread = lax.optimization_barrier((first_gates, second_spread))
    second_signal, second_outgoing = gather(second_spread)
    second_gates = exchange_gates(second_outgoing)
    first_turned = finish(first_signal, first_gates)
    first_turned, second_signal = lax.optimization_barrier((first_turned, second_signal))
    first_collected = forward_exchange(first_turned)
    second_turned = finish(second_signal, second_gates)
    second_collected = forward_exchange(second_turned)
    first_product = outer(first_vector, first_collected, False)
    first_product, second_collected = lax.optimization_barrier((first_product, second_collected))
    second_product = outer(second_vector, second_collected, False)
    return (first_product, second_product)


def solution(mesh):
    return step(mesh)


def step(mesh):
    return jax.shard_map(
        body,
        mesh=mesh,
        in_specs=(
            P(None, "freq", "node", None),
            P(None, "freq", "node", None),
            P(None, "freq", "node", None),
            P(),
            P("node", None),
            P("node", None, None, None),
            P("node", None, None, None),
        ),
        out_specs=(P(None, "freq", "node", None), P(None, "freq", "node", None)),
        check_vma=False,
    )
```

```python
import math

import jax
import jax.numpy as jnp
from jax import lax
from jax.experimental.layout import Layout, with_layout_constraint
from jax.sharding import PartitionSpec as P


dft_precision = lax.Precision.HIGH
mna_precision = lax.Precision.HIGH


def contract(form, left, right, precision):
    return jnp.einsum(form, left, right, precision=precision)


def cos_sin(first, second, length):
    angle = (first[:, None] * second[None, :] % length).astype(jnp.float32) * (
        2.0 * math.pi / length
    )
    return (jnp.cos(angle), jnp.sin(angle))


def body(
    first_vector, second_vector, conductance, terminals, pattern, conduct_blocks, capacit_blocks
):
    freq_count = lax.axis_size("freq")
    groups = lax.axis_size("node")
    local_bins = first_vector.shape[1]
    node_dev = first_vector.shape[2]
    inner_size = first_vector.shape[3]
    outer_size = local_bins * freq_count
    samples = outer_size * inner_size
    local_steps = inner_size // freq_count
    capacity = node_dev // groups
    freq_index = lax.axis_index("freq")
    node_index = lax.axis_index("node")
    bin_first = freq_index * local_bins + jnp.arange(local_bins, dtype=jnp.int32)
    step_first = freq_index * local_steps + jnp.arange(local_steps, dtype=jnp.int32)
    inner_range = jnp.arange(inner_size, dtype=jnp.int32)
    outer_range = jnp.arange(outer_size, dtype=jnp.int32)
    inner_cos, inner_sin = cos_sin(inner_range, inner_range, inner_size)
    outer_cos, outer_sin = cos_sin(outer_range, outer_range, outer_size)
    back_cos, back_sin = cos_sin(inner_range, bin_first, samples)
    fore_cos, fore_sin = cos_sin(step_first, outer_range, samples)
    scale = 1.0 / samples
    inv_inner = (
        jnp.stack([inner_cos, inner_sin], axis=1),
        jnp.stack([-inner_sin, inner_cos], axis=1),
    )
    inv_outer = (
        jnp.stack([outer_cos, outer_sin], axis=1) * scale,
        jnp.stack([-outer_sin, outer_cos], axis=1) * scale,
    )
    fwd_outer = (
        jnp.stack([outer_cos, -outer_sin], axis=1),
        jnp.stack([outer_sin, outer_cos], axis=1),
    )
    fwd_inner = (
        jnp.stack([inner_cos, -inner_sin], axis=1),
        jnp.stack([inner_sin, inner_cos], axis=1),
    )
    back_sign = jnp.array([-1.0, 1.0], jnp.float32)[:, None, None, None]
    fore_sign = jnp.array([1.0, -1.0], jnp.float32)[:, None, None, None]
    back_c = back_cos[None, :, :, None]
    back_s = back_sin[None, :, :, None] * back_sign
    fore_c = fore_cos[None, :, None, :]
    fore_s = fore_sin[None, :, None, :] * fore_sign

    node_ids = jnp.arange(node_dev, dtype=jnp.int32)
    turns = jnp.arange(groups, dtype=jnp.int32)
    recv_blocks = (node_index + turns) % groups
    send_blocks = (node_index - turns) % groups
    own_rows = lax.dynamic_slice_in_dim(terminals, node_index * node_dev, node_dev, 0)
    own_rot = own_rows.reshape(groups, capacity, 3)[recv_blocks].reshape(node_dev, 3)
    drain_hot = (own_rot[:, 0, None] == node_ids[None, :]).astype(jnp.float32)
    source_hot = (own_rot[:, 1, None] == node_ids[None, :]).astype(jnp.float32)
    incidence = drain_hot - source_hot
    arranged = terminals.reshape(groups, groups, capacity, 3)
    wanted = lax.dynamic_index_in_dim(arranged, node_index, axis=1, keepdims=False)
    wanted = wanted[send_blocks].reshape(node_dev, 3)
    gate_hot = (wanted[:, 2, None] == node_ids[None, :]).astype(jnp.float32)
    local_picks = jnp.concatenate([incidence, source_hot], axis=0)
    batch = (2, conductance.shape[1])
    gate_wide = jnp.broadcast_to(gate_hot, batch + gate_hot.shape)
    local_wide = jnp.broadcast_to(local_picks, batch + local_picks.shape)
    stamp_wide = jnp.broadcast_to(incidence.T, batch + incidence.T.shape)

    cond_blocks = conductance.reshape(
        conductance.shape[0], conductance.shape[1], groups, capacity, conductance.shape[3]
    )
    cond_rot = jnp.concatenate(
        [
            lax.dynamic_slice_in_dim(cond_blocks, recv_blocks[s], 1, axis=2)
            for s in range(groups)
        ],
        axis=2,
    ).reshape(conductance.shape)
    trans_g = cond_rot[0]
    output_g = cond_rot[1]

    block_size = conduct_blocks.shape[2]
    block_count = node_dev // block_size
    pattern_hot = (
        pattern[:, :, None] == jnp.arange(block_count, dtype=jnp.int32)[None, None, :]
    ).astype(jnp.float32)
    conduct_dense = contract(
        "bjc,bjrs->brcs", pattern_hot, conduct_blocks, lax.Precision.HIGHEST
    ).reshape(node_dev, node_dev)
    capacit_dense = contract(
        "bjc,bjrs->brcs", pattern_hot, capacit_blocks, lax.Precision.HIGHEST
    ).reshape(node_dev, node_dev)
    mna = jnp.stack([conduct_dense, capacit_dense])
    bin_index = bin_first[:, None] + outer_size * inner_range[None, :]
    signed = jnp.where(bin_index < samples // 2, bin_index, bin_index - samples)
    angular = (signed.astype(jnp.float32) * (2.0 * math.pi / samples))[:, None, :]

    def select(form, hot, values):
        return contract(form, hot, values, lax.Precision.HIGH)

    def complex_dft(form, parts, mats):
        return contract(form, parts[0], mats[0], dft_precision) + contract(
            form, parts[1], mats[1], dft_precision
        )

    def inner(vector):
        mixed = complex_dft("anb,bkm->kman", (vector[0], vector[1]), inv_inner)
        return mixed * back_c + mixed[::-1] * back_s

    def inverse_exchange(twisted):
        return lax.all_to_all(twisted, "freq", split_axis=1, concat_axis=2, tiled=True)

    def gather(spread):
        signal = complex_dft("man,akl->kmnl", (spread[0], spread[1]), inv_outer)
        return signal, select("kmdn,kmnl->kmdl", gate_wide, signal)

    def exchange_gates(outgoing):
        pieces = [outgoing[:, :, :capacity]]
        for s in range(1, groups):
            pieces.append(
                lax.ppermute(
                    outgoing[:, :, s * capacity : (s + 1) * capacity],
                    "node",
                    [(i, (i - s) % groups) for i in range(groups)],
                )
            )
        return jnp.concatenate(pieces, axis=2)

    def finish(signal, at_gate):
        picked = select("kmdn,kmnl->kmdl", local_wide, signal)
        drain_less_source = picked[:, :, :node_dev]
        at_source = picked[:, :, node_dev:]
        current = trans_g * (at_gate - at_source) + output_g * drain_less_source
        injected = select("kmnd,kmdl->kmnl", stamp_wide, current)
        turned = complex_dft("mnl,lka->kmna", (injected[0], injected[1]), fwd_outer)
        return turned * fore_c + turned[::-1] * fore_s

    def forward_exchange(twisted):
        return lax.all_to_all(twisted, "freq", split_axis=3, concat_axis=1, tiled=True)

    def outer(vector, collected, row_major):
        response = complex_dft("mna,mkb->kanb", (collected[0], collected[1]), fwd_inner)
        if row_major:
            response = with_layout_constraint(response, Layout(major_to_minor=(0, 1, 2, 3)))
        from_real = contract("jrs,asb->jarb", mna, vector[0], mna_precision)
        from_imag = contract("jrs,asb->jarb", mna, vector[1], mna_precision)
        return jnp.stack(
            [
                response[0] + from_real[0] - angular * from_imag[1],
                response[1] + from_imag[0] + angular * from_real[1],
            ]
        )

    first_twisted = inner(first_vector)
    first_twisted, second_held = lax.optimization_barrier((first_twisted, second_vector))
    first_spread = inverse_exchange(first_twisted)
    second_twisted = inner(second_held)
    second_spread = inverse_exchange(second_twisted)
    first_signal, first_outgoing = gather(first_spread)
    first_gates = exchange_gates(first_outgoing)
    first_gates, second_spread = lax.optimization_barrier((first_gates, second_spread))
    second_signal, second_outgoing = gather(second_spread)
    second_gates = exchange_gates(second_outgoing)
    first_turned = finish(first_signal, first_gates)
    first_turned, second_signal = lax.optimization_barrier((first_turned, second_signal))
    first_collected = forward_exchange(first_turned)
    second_turned = finish(second_signal, second_gates)
    second_collected = forward_exchange(second_turned)
    first_product = outer(first_vector, first_collected, True)
    first_product, second_collected = lax.optimization_barrier((first_product, second_collected))
    second_product = outer(second_vector, second_collected, False)
    return (first_product, second_product)


def solution(mesh):
    return step(mesh)


def step(mesh):
    return jax.shard_map(
        body,
        mesh=mesh,
        in_specs=(
            P(None, "freq", "node", None),
            P(None, "freq", "node", None),
            P(None, "freq", "node", None),
            P(),
            P("node", None),
            P("node", None, None, None),
            P("node", None, None, None),
        ),
        out_specs=(P(None, "freq", "node", None), P(None, "freq", "node", None)),
        check_vma=False,
    )
```
